256 devices in a mesh: coil: 8 (over z_hi, core), slab: 32 (over x, y, z_lo).
Axes of the slice: x: 4, y: 4, z: 8 (z_hi: 4, z_lo: 2; z = z_hi * 2 + z_lo), core: 2. Of those that a mesh axis runs over, the one named last changes fastest.
Arguments:
- image_field: float32 [2, 128, 192, 384], P(None, 'slab', 'coil'), may hold values from -6 to 6
- coil_maps: bfloat16 [2, 8, 128, 192, 384], P(None, 'coil', 'slab'), may hold values from -2 to 2
- kspace_data: bfloat16 [2, 8, 128, 192, 384], P(None, 'coil', None, 'slab'), may hold values from -6 to 6
- sampling_mask: int32 [128, 192], P(None, 'slab'), may hold values 0 or 1
- consistency_weight: float32 [1], replicated, may hold values from 0.5 to 2
- conv_first: bfloat16 [3, 3, 32, 3, 2], replicated, may hold values from -0.875 to 0.875
- conv_middle: bfloat16 [3, 3, 32, 3, 32], replicated, may hold values from -0.21875 to 0.21875
- conv_last: bfloat16 [3, 3, 2, 3, 32], replicated, may hold values from -0.21875 to 0.21875
Outputs:
- refined_image: float32 [2, 128, 192, 384], P(None, 'slab', 'coil')
The draws below stay inside these ranges and needn't reach their ends.
All inputs are finite; a program needn't handle non-finite values. No bound on the sum of `sampling_mask` on one device may be relied on, other than what follows from the above.
Results may differ from the reference program's by a relative error of at most 0.02.
Values may be sent and summed in bfloat16 or wider, within the bound.
No kernel may reach another device: no remote copies, remote signals or barrier semaphores. Data moves between devices by JAX's collectives and lax.ppermute only.
A program may use at most 128 MiB of HBM per device.

```python
import math
import jax
import jax.numpy as jnp
from jax import lax

READOUT = 384
PHASES = 192
PARTITIONS = 128
CHANNELS = 32
ALL_COILS = 8
N_SLAB = 32


def set_ends(array, own_key, low, largest):
    place = [jax.random.randint(jax.random.fold_in(own_key, axis), (), 0, length) for axis, length in enumerate(array.shape)]
    main_axis = array.shape.index(max(array.shape))
    next_to = place[:main_axis] + [(place[main_axis] + 1) % array.shape[main_axis]] + place[main_axis + 1:]
    return array.at[tuple(place)].set(low).at[tuple(next_to)].set(largest)


def strengthened(values, stream_key, source, target, parts, factor):
    owner, partner = [(jnp.arange(values.shape[dim]) // (values.shape[dim] // parts)).reshape([-1 if axis == dim else 1 for axis in range(values.ndim)]) for dim in (source, target)]
    chosen = jax.random.permutation(stream_key, parts)[partner]
    strong = (owner == chosen) | (owner == (partner + parts // 2) % parts)
    return jnp.where(strong, factor * values, values)


def block_scale(rng, extent, cuts, smallest, largest):
    def one(position, blocks):
        draws = jax.random.uniform(jax.random.fold_in(jax.random.fold_in(rng, 6), position), (blocks,), jnp.float32, smallest / len(cuts), largest / len(cuts))
        return jnp.repeat(jnp.exp(draws), extent[position] // blocks).reshape((-1,) + (1,) * (len(extent) - position - 1))

    loudness = one(*cuts[0])
    for cut in cuts[1:]:
        loudness = loudness * one(*cut)
    return loudness


def gaussian(stream_key, dims, spread, limit, cuts=(), kind=jnp.bfloat16):
    factor_of = block_scale(stream_key, dims, cuts, -0.22, 0.18) if cuts else 1.0
    values = jax.random.normal(stream_key, dims, jnp.float32) * spread * factor_of
    return jnp.minimum(jnp.maximum(values, -limit), limit).astype(kind)


def bell_draw_with(rng, extent, width, limit, cuts, heavy, kind=jnp.bfloat16):
    array = width * jax.random.normal(rng, extent, jnp.float32)
    if cuts:
        array = array * block_scale(rng, extent, cuts, -0.22, 0.18)
    return jnp.clip(strengthened(array, jax.random.fold_in(rng, 3), *heavy), -limit, limit).astype(kind)


def setup_inputs(seed: int = 0) -> dict:
    key_of = jax.random.split(jax.random.key(seed), 9)
    return {
        "image_field": gaussian(key_of[0], (2, PARTITIONS, PHASES, READOUT), 1.0, 6.0, ((1, 32), (2, 8)), jnp.float32),
        "coil_maps": bell_draw_with(key_of[1], (2, ALL_COILS, PARTITIONS, PHASES, READOUT), 0.25, 2.0, ((1, 8), (2, 32)), (1, 3, 8, 2.0)),
        "kspace_data": gaussian(key_of[2], (2, ALL_COILS, PARTITIONS, PHASES, READOUT), 1.0, 6.0, ((1, 8), (3, 32))),
        "sampling_mask": set_ends((jax.random.randint(key_of[3], (PARTITIONS, PHASES), 0, 2) < 1).astype(jnp.int32), jax.random.fold_in(key_of[3], 1), 0, 1),
        "consistency_weight": jnp.clip(jnp.exp(jax.random.uniform(key_of[4], (1,), jnp.float32, math.log(0.5), math.log(2.0))), 0.5, 2.0),
        "conv_first": gaussian(key_of[5], (3, 3, CHANNELS, 3, 2), 54 ** -0.5, 0.875),
        "conv_middle": gaussian(key_of[6], (3, 3, CHANNELS, 3, CHANNELS), (27 * CHANNELS) ** -0.5, 0.21875),
        "conv_last": gaussian(key_of[7], (3, 3, 2, 3, CHANNELS), (27 * CHANNELS) ** -0.5, 0.21875),
    }


def fourier_tables(length):
    points = jnp.arange(length, dtype=jnp.int32)
    product = points[:, None] * points[None, :] % length
    angles = product.astype(jnp.float32) * (2.0 * math.pi / length)
    scaling = 1.0 / math.sqrt(length)
    return jnp.stack([jnp.cos(angles) * scaling, jnp.sin(angles) * scaling]).astype(jnp.bfloat16)

def fourier_section(values, along, inverse):
    length = values.shape[along]
    matrices = fourier_tables(length).astype(jnp.float32)
    result = lax.dot_general(matrices, values.astype(jnp.float32), (((2,), (along,)), ((), ())), precision=lax.Precision.HIGHEST)
    result = jnp.moveaxis(result, 1, along + 1)
    cosine_part = result[0]
    sine_part = result[1]
    if inverse:
        real_part = cosine_part[0] - sine_part[1]
        imag_part = cosine_part[1] + sine_part[0]
    else:
        real_part = cosine_part[0] + sine_part[1]
        imag_part = cosine_part[1] - sine_part[0]
    return jnp.stack([real_part, imag_part]).astype(jnp.bfloat16)

def convolve(activations, weight):
    kernel = weight.astype(jnp.float32).transpose(2, 4, 0, 1, 3)
    return lax.conv_general_dilated(activations[None], kernel, (1, 1, 1), ((0, 0), (1, 1), (1, 1)), dimension_numbers=('NCDHW', 'OIDHW', 'NCDHW'), precision=lax.Precision.HIGHEST)[0]

def regularize(pixels, conv_first, conv_middle, conv_last):
    block_rows = PARTITIONS // N_SLAB
    padded = jnp.pad(pixels, ((0, 0), (3, 3), (0, 0), (0, 0)))

    def inside(first_row, row_count):
        places = first_row + jnp.arange(row_count, dtype=jnp.int32)
        return ((places >= 0) & (places < PARTITIONS)).astype(jnp.float32)[None, :, None, None]

    def one_block(block_index):
        first_row = block_index * block_rows
        window = lax.dynamic_slice_in_dim(padded, first_row, block_rows + 6, 1)
        window = lax.optimization_barrier(window).astype(jnp.float32)
        hidden_one = jax.nn.relu(convolve(window, conv_first)) * inside(first_row - 2, block_rows + 4)
        hidden_one = lax.optimization_barrier(hidden_one.astype(jnp.bfloat16)).astype(jnp.float32)
        hidden_two = jax.nn.relu(convolve(hidden_one, conv_middle)) * inside(first_row - 1, block_rows + 2)
        hidden_two = lax.optimization_barrier(hidden_two.astype(jnp.bfloat16)).astype(jnp.float32)
        return convolve(hidden_two, conv_last)
    pieces = lax.map(one_block, jnp.arange(N_SLAB, dtype=jnp.int32))
    return jnp.moveaxis(pieces, 0, 1).reshape(2, PARTITIONS, PHASES, READOUT)

def reference(image_field, coil_maps, kspace_data, sampling_mask, consistency_weight, conv_first, conv_middle, conv_last):
    pixels = lax.optimization_barrier(image_field.astype(jnp.bfloat16)).astype(jnp.float32)
    weights_mask = sampling_mask.astype(jnp.float32)[None, :, :, None]

    def per_coil(summed, inputs):
        sensitivity, measured = inputs
        sensitivity = sensitivity.astype(jnp.float32)
        expanded = jnp.stack([sensitivity[0] * pixels[0] - sensitivity[1] * pixels[1], sensitivity[0] * pixels[1] + sensitivity[1] * pixels[0]]).astype(jnp.bfloat16)
        spectrum = fourier_section(expanded, 3, False)
        spectrum = fourier_section(spectrum, 2, False)
        spectrum = fourier_section(spectrum, 1, False)
        residual = (weights_mask * (spectrum.astype(jnp.float32) - measured.astype(jnp.float32))).astype(jnp.bfloat16)
        restored = fourier_section(residual, 1, True)
        restored = fourier_section(restored, 2, True)
        restored = fourier_section(restored, 3, True).astype(jnp.float32)
        contribution = jnp.stack([sensitivity[0] * restored[0] + sensitivity[1] * restored[1], sensitivity[0] * restored[1] - sensitivity[1] * restored[0]])
        return (summed + contribution, None)
    initial = jnp.zeros((2, PARTITIONS, PHASES, READOUT), jnp.float32)
    gradient, _ = lax.scan(per_coil, initial, (jnp.moveaxis(coil_maps, 1, 0), jnp.moveaxis(kspace_data, 1, 0)))
    updated = image_field - consistency_weight[0] * gradient
    correction = regularize(updated.astype(jnp.bfloat16), conv_first, conv_middle, conv_last)
    return updated + correction
```

```python
import math

import jax
import jax.numpy as jnp
from jax import lax
from jax.sharding import PartitionSpec as P


def padded_2(block, sides, width):
    for axis, dim in sides:
        count = lax.axis_size(axis)
        forward = [(i, i + 1) for i in range(count - 1)]
        backward = [(target, source) for source, target in forward]
        low = lax.ppermute(
            lax.slice_in_dim(block, block.shape[dim] - width, None, axis=dim), axis, forward
        )
        high = lax.ppermute(lax.slice_in_dim(block, 0, width, axis=dim), axis, backward)
        block = jnp.concatenate([low, block, high], axis=dim)
    return block


def fourier_tables(length):
    points = jnp.arange(length, dtype=jnp.int32)
    product = points[:, None] * points[None, :] % length
    angles = product.astype(jnp.float32) * (2.0 * math.pi / length)
    scaling = 1.0 / math.sqrt(length)
    return jnp.stack([jnp.cos(angles) * scaling, jnp.sin(angles) * scaling]).astype(jnp.bfloat16)


def fourier_section(values, along, inverse):
    length = values.shape[along]
    tables = fourier_tables(length)
    cosine = tables[0]
    sine = -tables[1] if inverse else tables[1]
    matrix = jnp.stack([jnp.stack([cosine, sine], axis=1), jnp.stack([-sine, cosine], axis=1)])
    result = lax.dot_general(
        matrix, values, (((2, 3), (0, along)), ((), ())), preferred_element_type=jnp.float32
    )
    result = jnp.moveaxis(result, 1, along)
    return result.astype(jnp.bfloat16)


def convolve(activations, weight):
    kernel = weight.transpose(2, 4, 0, 1, 3)
    return lax.conv_general_dilated(
        activations[None],
        kernel,
        (1, 1, 1),
        ((0, 0), (0, 0), (1, 1)),
        dimension_numbers=("NCDHW", "OIDHW", "NCDHW"),
        preferred_element_type=jnp.float32,
    )[0]


def inside_mask(depth_first, depth_count, row_first, row_count, depth_limit, row_limit):
    depth_places = depth_first + jnp.arange(depth_count, dtype=jnp.int32)
    row_places = row_first + jnp.arange(row_count, dtype=jnp.int32)
    depth_inside = (depth_places >= 0) & (depth_places < depth_limit)
    row_inside = (row_places >= 0) & (row_places < row_limit)
    return (depth_inside[:, None] & row_inside[None, :]).astype(jnp.float32)[None, :, :, None]


def per_device(
    image_field,
    coil_maps,
    kspace_data,
    sampling_mask,
    consistency_weight,
    conv_first,
    conv_middle,
    conv_last,
):
    slab_rows = image_field.shape[1]
    coil_rows = image_field.shape[2]
    phases = coil_maps.shape[3]
    partitions = kspace_data.shape[2]
    pixels = image_field.astype(jnp.bfloat16)
    sensitivity = coil_maps.astype(jnp.float32)
    values = lax.all_gather(pixels, "coil", axis=2, tiled=True).astype(jnp.float32)[:, None]
    expanded = jnp.stack(
        [
            sensitivity[0] * values[0] - sensitivity[1] * values[1],
            sensitivity[0] * values[1] + sensitivity[1] * values[0],
        ]
    ).astype(jnp.bfloat16)
    spectrum = fourier_section(expanded, 4, False)
    spectrum = fourier_section(spectrum, 3, False)
    spectrum = lax.all_to_all(spectrum, "slab", split_axis=3, concat_axis=2, tiled=True)
    spectrum = fourier_section(spectrum, 2, False)
    weights_mask = sampling_mask.astype(jnp.float32)[None, None, :, :, None]
    residual = (
        weights_mask * (spectrum.astype(jnp.float32) - kspace_data.astype(jnp.float32))
    ).astype(jnp.bfloat16)
    residual = fourier_section(residual, 2, True)
    residual = lax.all_to_all(residual, "slab", split_axis=2, concat_axis=3, tiled=True)
    residual = fourier_section(residual, 3, True)
    restored = fourier_section(residual, 4, True).astype(jnp.float32)
    sensitivity = coil_maps.astype(jnp.float32)
    partial_value = jnp.stack(
        [
            jnp.sum(sensitivity[0] * restored[0] + sensitivity[1] * restored[1], axis=0),
            jnp.sum(sensitivity[0] * restored[1] - sensitivity[1] * restored[0], axis=0),
        ]
    )
    step_size = consistency_weight[0]
    coil_first = lax.axis_index("coil") * coil_rows
    slab_first = lax.axis_index("slab") * slab_rows
    weights = (conv_first, conv_middle, conv_last)
    scattered = lax.psum_scatter(
        (-step_size * partial_value).astype(jnp.bfloat16), "coil", scatter_dimension=2, tiled=True
    )
    updated = image_field + scattered.astype(jnp.float32)
    activations = padded_2(updated.astype(jnp.bfloat16), (("coil", 2),), 3)
    for layer_index, weight in enumerate(weights):
        extended = padded_2(activations, (("slab", 1),), 1)
        output = convolve(extended, weight)
        if layer_index < 2:
            margin = 2 - layer_index
            inside = inside_mask(
                slab_first,
                output.shape[1],
                coil_first - margin,
                output.shape[2],
                partitions,
                phases,
            )
            activations = (jax.nn.relu(output) * inside).astype(jnp.bfloat16)
    return updated + output


def solution(mesh):
    placed = (
        P(None, "slab", "coil", None),
        P(None, "coil", "slab", None, None),
        P(None, "coil", None, "slab", None),
        P(None, "slab"),
        P(),
        P(),
        P(),
        P(),
    )
    return jax.shard_map(
        per_device,
        mesh=mesh,
        in_specs=placed,
        out_specs=P(None, "slab", "coil", None),
        check_vma=False,
    )
```

```python
import math

import jax
import jax.numpy as jnp
from jax import lax
from jax.sharding import PartitionSpec as P


def padded_2(block, sides, width):
    for axis, dim in sides:
        count = lax.axis_size(axis)
        forward = [(i, i + 1) for i in range(count - 1)]
        backward = [(target, source) for source, target in forward]
        low = lax.ppermute(
            lax.slice_in_dim(block, block.shape[dim] - width, None, axis=dim), axis, forward
        )
        high = lax.ppermute(lax.slice_in_dim(block, 0, width, axis=dim), axis, backward)
        block = jnp.concatenate([low, block, high], axis=dim)
    return block


def fourier_tables(length):
    points = jnp.arange(length, dtype=jnp.int32)
    product = points[:, None] * points[None, :] % length
    angles = product.astype(jnp.float32) * (2.0 * math.pi / length)
    scaling = 1.0 / math.sqrt(length)
    return jnp.stack([jnp.cos(angles) * scaling, jnp.sin(angles) * scaling]).astype(jnp.bfloat16)


def fourier_section(values, along, inverse):
    length = values.shape[along]
    tables = fourier_tables(length)
    cosine = tables[0]
    sine = -tables[1] if inverse else tables[1]
    matrix = jnp.stack([jnp.stack([cosine, sine], axis=1), jnp.stack([-sine, cosine], axis=1)])
    result = lax.dot_general(
        matrix, values, (((2, 3), (0, along)), ((), ())), preferred_element_type=jnp.float32
    )
    result = jnp.moveaxis(result, 1, along)
    return result.astype(jnp.bfloat16)


def convolve(activations, weight):
    in_channels = activations.shape[0]
    out_depth = activations.shape[1] - 2
    out_rows = activations.shape[2] - 2
    readout = activations.shape[3]
    padded = jnp.pad(activations, ((0, 0), (0, 0), (0, 0), (1, 1)))
    shifted = jnp.concatenate(
        [padded[..., 0:readout], padded[..., 1 : readout + 1], padded[..., 2 : readout + 2]], axis=0
    )
    summed = None
    for depth_step in range(3):
        for row_step in range(3):
            kernel = weight[depth_step, row_step].reshape(weight.shape[2], 3 * in_channels)
            contribution = jnp.einsum(
                "ok,kzyx->ozyx",
                kernel,
                shifted[:, depth_step : depth_step + out_depth, row_step : row_step + out_rows, :],
                preferred_element_type=jnp.float32,
            )
            summed = contribution if summed is None else summed + contribution
    return summed


def inside_mask(depth_first, depth_count, row_first, row_count, depth_limit, row_limit):
    depth_places = depth_first + jnp.arange(depth_count, dtype=jnp.int32)
    row_places = row_first + jnp.arange(row_count, dtype=jnp.int32)
    depth_inside = (depth_places >= 0) & (depth_places < depth_limit)
    row_inside = (row_places >= 0) & (row_places < row_limit)
    return (depth_inside[:, None] & row_inside[None, :]).astype(jnp.float32)[None, :, :, None]


def per_device(
    image_field,
    coil_maps,
    kspace_data,
    sampling_mask,
    consistency_weight,
    conv_first,
    conv_middle,
    conv_last,
):
    slab_rows = image_field.shape[1]
    coil_rows = image_field.shape[2]
    phases = coil_maps.shape[3]
    partitions = kspace_data.shape[2]
    pixels = image_field.astype(jnp.bfloat16)
    sensitivity = coil_maps.astype(jnp.float32)
    values = lax.all_gather(pixels, "coil", axis=2, tiled=True).astype(jnp.float32)[:, None]
    expanded = jnp.stack(
        [
            sensitivity[0] * values[0] - sensitivity[1] * values[1],
            sensitivity[0] * values[1] + sensitivity[1] * values[0],
        ]
    ).astype(jnp.bfloat16)
    spectrum = fourier_section(expanded, 4, False)
    spectrum = fourier_section(spectrum, 3, False)
    spectrum = lax.all_to_all(spectrum, "slab", split_axis=3, concat_axis=2, tiled=True)
    spectrum = fourier_section(spectrum, 2, False)
    weights_mask = sampling_mask.astype(jnp.float32)[None, None, :, :, None]
    residual = (
        weights_mask * (spectrum.astype(jnp.float32) - kspace_data.astype(jnp.float32))
    ).astype(jnp.bfloat16)
    residual = fourier_section(residual, 2, True)
    residual = lax.all_to_all(residual, "slab", split_axis=2, concat_axis=3, tiled=True)
    residual = fourier_section(residual, 3, True)
    restored = fourier_section(residual, 4, True).astype(jnp.float32)
    sensitivity = coil_maps.astype(jnp.float32)
    partial_value = jnp.stack(
        [
            jnp.sum(sensitivity[0] * restored[0] + sensitivity[1] * restored[1], axis=0),
            jnp.sum(sensitivity[0] * restored[1] - sensitivity[1] * restored[0], axis=0),
        ]
    )
    step_size = consistency_weight[0]
    coil_first = lax.axis_index("coil") * coil_rows
    slab_first = lax.axis_index("slab") * slab_rows
    weights = (conv_first, conv_middle, conv_last)
    scattered = lax.psum_scatter(
        (-step_size * partial_value).astype(jnp.bfloat16), "coil", scatter_dimension=2, tiled=True
    )
    updated = image_field + scattered.astype(jnp.float32)
    activations = padded_2(updated.astype(jnp.bfloat16), (("coil", 2),), 3)
    for layer_index, weight in enumerate(weights):
        extended = padded_2(activations, (("slab", 1),), 1)
        output = convolve(extended, weight)
        if layer_index < 2:
            margin = 2 - layer_index
            inside = inside_mask(
                slab_first,
                output.shape[1],
                coil_first - margin,
                output.shape[2],
                partitions,
                phases,
            )
            activations = (jax.nn.relu(output) * inside).astype(jnp.bfloat16)
    return updated + output


def solution(mesh):
    placed = (
        P(None, "slab", "coil", None),
        P(None, "coil", "slab", None, None),
        P(None, "coil", None, "slab", None),
        P(None, "slab"),
        P(),
        P(),
        P(),
        P(),
    )
    return jax.shard_map(
        per_device,
        mesh=mesh,
        in_specs=placed,
        out_specs=P(None, "slab", "coil", None),
        check_vma=False,
    )
```

```python
import math

import jax
import jax.numpy as jnp
from jax import lax
from jax.experimental import pallas as pl
from jax.sharding import PartitionSpec as P


def padded_2(block, sides, width):
    for axis, dim in sides:
        count = lax.axis_size(axis)
        forward = [(i, i + 1) for i in range(count - 1)]
        backward = [(target, source) for source, target in forward]
        low = lax.ppermute(
            lax.slice_in_dim(block, block.shape[dim] - width, None, axis=dim), axis, forward
        )
        high = lax.ppermute(lax.slice_in_dim(block, 0, width, axis=dim), axis, backward)
        block = jnp.concatenate([low, block, high], axis=dim)
    return block


def fourier_tables(length):
    points = jnp.arange(length, dtype=jnp.int32)
    product = points[:, None] * points[None, :] % length
    angles = product.astype(jnp.float32) * (2.0 * math.pi / length)
    scaling = 1.0 / math.sqrt(length)
    return jnp.stack([jnp.cos(angles) * scaling, jnp.sin(angles) * scaling]).astype(jnp.bfloat16)


def fourier_section(values, along, inverse):
    length = values.shape[along]
    tables = fourier_tables(length)
    cosine = tables[0]
    sine = -tables[1] if inverse else tables[1]
    matrix = jnp.stack([jnp.stack([cosine, sine], axis=1), jnp.stack([-sine, cosine], axis=1)])
    result = lax.dot_general(
        matrix, values, (((2, 3), (0, along)), ((), ())), preferred_element_type=jnp.float32
    )
    result = jnp.moveaxis(result, 1, along)
    return result.astype(jnp.bfloat16)


READ = 384
CHUNK = 768

def conv_flat(stack, kernel, out_rows):
    depth_in, width, lanes_in = stack.shape
    out_depth = depth_in - 2
    out_channels = kernel.shape[2]
    lanes = out_rows * READ
    steps = lanes // CHUNK

    def body(s0, s1, s2, w_ref, o_ref):
        sources = (s0, s1, s2)

        def chunk(index, carry):
            start = pl.multiple_of(index * CHUNK, 128)
            acc = jnp.zeros((out_channels, CHUNK), jnp.float32)
            for dz in range(3):
                for dy in range(3):
                    acc = acc + jnp.dot(
                        w_ref[dz, dy],
                        sources[dz][0, :, pl.ds(start + dy * READ, CHUNK)],
                        preferred_element_type=jnp.float32,
                    )
            o_ref[0, :, pl.ds(start, CHUNK)] = acc
            return carry

        lax.fori_loop(0, steps, chunk, 0)

    in_specs = [
        pl.BlockSpec((1, width, lanes_in), lambda z, dz=dz: (z + dz, 0, 0)) for dz in range(3)
    ] + [pl.BlockSpec(kernel.shape, lambda z: (0, 0, 0, 0))]
    return pl.pallas_call(
        body,
        grid=(out_depth,),
        in_specs=in_specs,
        out_specs=pl.BlockSpec((1, out_channels, lanes), lambda z: (z, 0, 0)),
        out_shape=jax.ShapeDtypeStruct((out_depth, out_channels, lanes), jnp.float32),
    )(stack, stack, stack, kernel)


def shifted_stack(block):
    channels = block.shape[1]
    left = jnp.pad(block, ((0, 0), (0, 0), (1, 0)))[..., :-1]
    right = jnp.pad(block, ((0, 0), (0, 0), (0, 1)))[..., 1:]
    place = lax.broadcasted_iota(jnp.int32, block.shape, 2) % READ
    zero = jnp.zeros((), block.dtype)
    left = jnp.where(place == 0, zero, left)
    right = jnp.where(place == READ - 1, zero, right)
    pieces = [left, block, right]
    extra = -(3 * channels) % 16
    if extra:
        pieces.append(jnp.zeros(block.shape[:1] + (extra,) + block.shape[2:], block.dtype))
    return jnp.concatenate(pieces, axis=1)


def kernel_matrix(weight):
    out_channels, in_channels = weight.shape[2], weight.shape[4]
    matrix = weight.reshape(3, 3, out_channels, 3 * in_channels)
    extra_in = -(3 * in_channels) % 16
    extra_out = -out_channels % 8
    return jnp.pad(matrix, ((0, 0), (0, 0), (0, extra_out), (0, extra_in)))


def convolve_flat(block, weight, out_rows):
    out = conv_flat(shifted_stack(block), kernel_matrix(weight), out_rows)
    return out[:, : weight.shape[2]]


def per_device(
    image_field,
    coil_maps,
    kspace_data,
    sampling_mask,
    consistency_weight,
    conv_first,
    conv_middle,
    conv_last,
):
    slab_rows = image_field.shape[1]
    coil_rows = image_field.shape[2]
    phases = coil_maps.shape[3]
    partitions = kspace_data.shape[2]
    pixels = image_field.astype(jnp.bfloat16)
    sensitivity = coil_maps.astype(jnp.float32)
    values = lax.all_gather(pixels, "coil", axis=2, tiled=True).astype(jnp.float32)[:, None]
    expanded = jnp.stack(
        [
            sensitivity[0] * values[0] - sensitivity[1] * values[1],
            sensitivity[0] * values[1] + sensitivity[1] * values[0],
        ]
    ).astype(jnp.bfloat16)
    spectrum = fourier_section(expanded, 4, False)
    spectrum = fourier_section(spectrum, 3, False)
    spectrum = lax.all_to_all(spectrum, "slab", split_axis=3, concat_axis=2, tiled=True)
    spectrum = fourier_section(spectrum, 2, False)
    weights_mask = sampling_mask.astype(jnp.float32)[None, None, :, :, None]
    residual = (
        weights_mask * (spectrum.astype(jnp.float32) - kspace_data.astype(jnp.float32))
    ).astype(jnp.bfloat16)
    residual = fourier_section(residual, 2, True)
    residual = lax.all_to_all(residual, "slab", split_axis=2, concat_axis=3, tiled=True)
    residual = fourier_section(residual, 3, True)
    restored = fourier_section(residual, 4, True).astype(jnp.float32)
    sensitivity = coil_maps.astype(jnp.float32)
    partial_value = jnp.stack(
        [
            jnp.sum(sensitivity[0] * restored[0] + sensitivity[1] * restored[1], axis=0),
            jnp.sum(sensitivity[0] * restored[1] - sensitivity[1] * restored[0], axis=0),
        ]
    )
    step_size = consistency_weight[0]
    coil_first = lax.axis_index("coil") * coil_rows
    slab_first = lax.axis_index("slab") * slab_rows
    weights = (conv_first, conv_middle, conv_last)
    scattered = lax.psum_scatter(
        (-step_size * partial_value).astype(jnp.bfloat16), "coil", scatter_dimension=2, tiled=True
    )
    updated = image_field + scattered.astype(jnp.float32)
    activations = padded_2(updated.astype(jnp.bfloat16), (("coil", 2),), 3)
    rows = activations.shape[2]
    activations = activations.transpose(1, 0, 2, 3).reshape(slab_rows, 2, rows * READ)
    for layer_index, weight in enumerate(weights):
        extended = padded_2(activations, (("slab", 0),), 1)
        rows = rows - 2
        output = convolve_flat(extended, weight, rows)
        if layer_index < 2:
            margin = 2 - layer_index
            depth_places = slab_first + jnp.arange(slab_rows, dtype=jnp.int32)
            row_places = coil_first - margin + jnp.arange(rows * READ, dtype=jnp.int32) // READ
            inside = (
                ((depth_places >= 0) & (depth_places < partitions))[:, None, None]
                & ((row_places >= 0) & (row_places < phases))[None, None, :]
            )
            activations = jnp.where(inside, jax.nn.relu(output), 0.0).astype(jnp.bfloat16)
    correction = output.reshape(slab_rows, 2, coil_rows, READ).transpose(1, 0, 2, 3)
    return updated + correction


def solution(mesh):
    placed = (
        P(None, "slab", "coil", None),
        P(None, "coil", "slab", None, None),
        P(None, "coil", None, "slab", None),
        P(None, "slab"),
        P(),
        P(),
        P(),
        P(),
    )
    return jax.shard_map(
        per_device,
        mesh=mesh,
        in_specs=placed,
        out_specs=P(None, "slab", "coil", None),
        check_vma=False,
    )
```

```python
import math

import jax
import jax.numpy as jnp
from jax import lax
from jax.experimental import pallas as pl
from jax.sharding import PartitionSpec as P


def padded_2(block, sides, width):
    for axis, dim in sides:
        count = lax.axis_size(axis)
        forward = [(i, i + 1) for i in range(count - 1)]
        backward = [(target, source) for source, target in forward]
        low = lax.ppermute(
            lax.slice_in_dim(block, block.shape[dim] - width, None, axis=dim), axis, forward
        )
        high = lax.ppermute(lax.slice_in_dim(block, 0, width, axis=dim), axis, backward)
        block = jnp.concatenate([low, block, high], axis=dim)
    return block


def fourier_tables(length):
    points = jnp.arange(length, dtype=jnp.int32)
    product = points[:, None] * points[None, :] % length
    angles = product.astype(jnp.float32) * (2.0 * math.pi / length)
    scaling = 1.0 / math.sqrt(length)
    return jnp.stack([jnp.cos(angles) * scaling, jnp.sin(angles) * scaling]).astype(jnp.bfloat16)


def fourier_section(values, along, inverse):
    length = values.shape[along]
    tables = fourier_tables(length)
    cosine = tables[0]
    sine = -tables[1] if inverse else tables[1]
    matrix = jnp.stack([jnp.stack([cosine, sine], axis=1), jnp.stack([-sine, cosine], axis=1)])
    result = lax.dot_general(
        matrix, values, (((2, 3), (0, along)), ((), ())), preferred_element_type=jnp.float32
    )
    result = jnp.moveaxis(result, 1, along)
    return result.astype(jnp.bfloat16)


READ = 384
CHUNK = 768

def conv_flat(stack, kernel, out_rows):
    depth_in, width, lanes_in = stack.shape
    out_depth = depth_in - 2
    out_channels = kernel.shape[2]
    lanes = out_rows * READ
    steps = lanes // CHUNK

    def body(s0, s1, s2, w_ref, o_ref):
        sources = (s0, s1, s2)

        def chunk(index, carry):
            start = pl.multiple_of(index * CHUNK, 128)
            acc = jnp.zeros((out_channels, CHUNK), jnp.float32)
            for dz in range(3):
                for dy in range(3):
                    acc = acc + jnp.dot(
                        w_ref[dz, dy],
                        sources[dz][0, :, pl.ds(start + dy * READ, CHUNK)],
                        preferred_element_type=jnp.float32,
                    )
            o_ref[0, :, pl.ds(start, CHUNK)] = acc
            return carry

        lax.fori_loop(0, steps, chunk, 0)

    in_specs = [
        pl.BlockSpec((1, width, lanes_in), lambda z, dz=dz: (z + dz, 0, 0)) for dz in range(3)
    ] + [pl.BlockSpec(kernel.shape, lambda z: (0, 0, 0, 0))]
    return pl.pallas_call(
        body,
        grid=(out_depth,),
        in_specs=in_specs,
        out_specs=pl.BlockSpec((1, out_channels, lanes), lambda z: (z, 0, 0)),
        out_shape=jax.ShapeDtypeStruct((out_depth, out_channels, lanes), jnp.float32),
    )(stack, stack, stack, kernel)


def shifted_stack(block):
    channels = block.shape[1]
    left = jnp.pad(block, ((0, 0), (0, 0), (1, 0)))[..., :-1]
    right = jnp.pad(block, ((0, 0), (0, 0), (0, 1)))[..., 1:]
    place = lax.broadcasted_iota(jnp.int32, block.shape, 2) % READ
    zero = jnp.zeros((), block.dtype)
    left = jnp.where(place == 0, zero, left)
    right = jnp.where(place == READ - 1, zero, right)
    pieces = [left, block, right]
    extra = -(3 * channels) % 16
    if extra:
        pieces.append(jnp.zeros(block.shape[:1] + (extra,) + block.shape[2:], block.dtype))
    return jnp.concatenate(pieces, axis=1)


def kernel_matrix(weight):
    out_channels, in_channels = weight.shape[2], weight.shape[4]
    matrix = weight.reshape(3, 3, out_channels, 3 * in_channels)
    extra_in = -(3 * in_channels) % 16
    extra_out = -out_channels % 8
    return jnp.pad(matrix, ((0, 0), (0, 0), (0, extra_out), (0, extra_in)))


def convolve_flat(block, weight, out_rows):
    out = conv_flat(shifted_stack(block), kernel_matrix(weight), out_rows)
    return out[:, : weight.shape[2]]


def per_device(
    image_field,
    coil_maps,
    kspace_data,
    sampling_mask,
    consistency_weight,
    conv_first,
    conv_middle,
    conv_last,
):
    slab_rows = image_field.shape[1]
    coil_rows = image_field.shape[2]
    phases = coil_maps.shape[3]
    partitions = kspace_data.shape[2]
    pixels = image_field.astype(jnp.bfloat16)
    sensitivity = coil_maps.astype(jnp.float32)
    values = lax.all_gather(pixels, "coil", axis=2, tiled=True).astype(jnp.float32)[:, None]
    expanded = jnp.stack(
        [
            sensitivity[0] * values[0] - sensitivity[1] * values[1],
            sensitivity[0] * values[1] + sensitivity[1] * values[0],
        ]
    ).astype(jnp.bfloat16)
    spectrum = fourier_section(expanded, 4, False)
    spectrum = fourier_section(spectrum, 3, False)
    spectrum = lax.all_to_all(spectrum, "slab", split_axis=3, concat_axis=2, tiled=True)
    spectrum = fourier_section(spectrum, 2, False)
    weights_mask = sampling_mask.astype(jnp.float32)[None, None, :, :, None]
    residual = (
        weights_mask * (spectrum.astype(jnp.float32) - kspace_data.astype(jnp.float32))
    ).astype(jnp.bfloat16)
    residual = fourier_section(residual, 2, True)
    residual = lax.all_to_all(residual, "slab", split_axis=2, concat_axis=3, tiled=True)
    residual = fourier_section(residual, 3, True)
    restored = fourier_section(residual, 4, True).astype(jnp.float32)
    sensitivity = coil_maps.astype(jnp.float32)
    partial_value = jnp.stack(
        [
            jnp.sum(sensitivity[0] * restored[0] + sensitivity[1] * restored[1], axis=0),
            jnp.sum(sensitivity[0] * restored[1] - sensitivity[1] * restored[0], axis=0),
        ]
    )
    step_size = consistency_weight[0]
    coil_first = lax.axis_index("coil") * coil_rows
    slab_first = lax.axis_index("slab") * slab_rows
    weights = (conv_first, conv_middle, conv_last)
    scattered = lax.psum_scatter(
        (-step_size * partial_value).astype(jnp.bfloat16), "coil", scatter_dimension=2, tiled=True
    )
    updated = image_field + scattered.astype(jnp.float32)
    activations = padded_2(updated.astype(jnp.bfloat16), (("coil", 2),), 3)
    activations = padded_2(activations, (("slab", 1),), 3)
    depth, rows = activations.shape[1], activations.shape[2]
    activations = activations.transpose(1, 0, 2, 3).reshape(depth, 2, rows * READ)
    for layer_index, weight in enumerate(weights):
        rows = rows - 2
        output = convolve_flat(activations, weight, rows)
        if layer_index < 2:
            margin = 2 - layer_index
            depth_places = slab_first - margin + jnp.arange(output.shape[0], dtype=jnp.int32)
            row_places = coil_first - margin + jnp.arange(rows * READ, dtype=jnp.int32) // READ
            inside = (
                ((depth_places >= 0) & (depth_places < partitions))[:, None, None]
                & ((row_places >= 0) & (row_places < phases))[None, None, :]
            )
            activations = jnp.where(inside, jax.nn.relu(output), 0.0).astype(jnp.bfloat16)
    correction = output.reshape(slab_rows, 2, coil_rows, READ).transpose(1, 0, 2, 3)
    return updated + correction


def solution(mesh):
    placed = (
        P(None, "slab", "coil", None),
        P(None, "coil", "slab", None, None),
        P(None, "coil", None, "slab", None),
        P(None, "slab"),
        P(),
        P(),
        P(),
        P(),
    )
    return jax.shard_map(
        per_device,
        mesh=mesh,
        in_specs=placed,
        out_specs=P(None, "slab", "coil", None),
        check_vma=False,
    )
```

```python
import math

import jax
import jax.numpy as jnp
from jax import lax
from jax.experimental import pallas as pl
from jax.sharding import PartitionSpec as P


def padded_2(block, sides, width):
    for axis, dim in sides:
        count = lax.axis_size(axis)
        forward = [(i, i + 1) for i in range(count - 1)]
        backward = [(target, source) for source, target in forward]
        low = lax.ppermute(
            lax.slice_in_dim(block, block.shape[dim] - width, None, axis=dim), axis, forward
        )
        high = lax.ppermute(lax.slice_in_dim(block, 0, width, axis=dim), axis, backward)
        block = jnp.concatenate([low, block, high], axis=dim)
    return block


def fourier_tables(length):
    points = jnp.arange(length, dtype=jnp.int32)
    product = points[:, None] * points[None, :] % length
    angles = product.astype(jnp.float32) * (2.0 * math.pi / length)
    scaling = 1.0 / math.sqrt(length)
    return jnp.stack([jnp.cos(angles) * scaling, jnp.sin(angles) * scaling]).astype(jnp.bfloat16)


def fourier_section(values, along, inverse):
    length = values.shape[along]
    tables = fourier_tables(length)
    cosine = tables[0]
    sine = -tables[1] if inverse else tables[1]
    matrix = jnp.stack([jnp.stack([cosine, sine], axis=1), jnp.stack([-sine, cosine], axis=1)])
    result = lax.dot_general(
        matrix, values, (((2, 3), (0, along)), ((), ())), preferred_element_type=jnp.float32
    )
    result = jnp.moveaxis(result, 1, along)
    return result.astype(jnp.bfloat16)


READ = 384
CHUNK = 1536

def conv_flat(stack, kernel, out_rows):
    depth_in, width, lanes_in = stack.shape
    out_depth = depth_in - 2
    out_channels = kernel.shape[2]
    lanes = out_rows * READ
    starts = range(0, lanes, CHUNK)

    def body(s0, s1, s2, w_ref, o_ref):
        sources = (s0, s1, s2)
        for start in starts:
            size = min(CHUNK, lanes - start)
            acc = jnp.zeros((out_channels, size), jnp.float32)
            for dz in range(3):
                for dy in range(3):
                    acc = acc + jnp.dot(
                        w_ref[dz, dy],
                        sources[dz][0, :, pl.ds(start + dy * READ, size)],
                        preferred_element_type=jnp.float32,
                    )
            o_ref[0, :, pl.ds(start, size)] = acc

    in_specs = [
        pl.BlockSpec((1, width, lanes_in), lambda z, dz=dz: (z + dz, 0, 0)) for dz in range(3)
    ] + [pl.BlockSpec(kernel.shape, lambda z: (0, 0, 0, 0))]
    return pl.pallas_call(
        body,
        grid=(out_depth,),
        in_specs=in_specs,
        out_specs=pl.BlockSpec((1, out_channels, lanes), lambda z: (z, 0, 0)),
        out_shape=jax.ShapeDtypeStruct((out_depth, out_channels, lanes), jnp.float32),
    )(stack, stack, stack, kernel)


def shifted_stack(block):
    channels = block.shape[1]
    left = jnp.pad(block, ((0, 0), (0, 0), (1, 0)))[..., :-1]
    right = jnp.pad(block, ((0, 0), (0, 0), (0, 1)))[..., 1:]
    place = lax.broadcasted_iota(jnp.int32, block.shape, 2) % READ
    zero = jnp.zeros((), block.dtype)
    left = jnp.where(place == 0, zero, left)
    right = jnp.where(place == READ - 1, zero, right)
    pieces = [left, block, right]
    extra = -(3 * channels) % 16
    if extra:
        pieces.append(jnp.zeros(block.shape[:1] + (extra,) + block.shape[2:], block.dtype))
    return jnp.concatenate(pieces, axis=1)


def kernel_matrix(weight):
    out_channels, in_channels = weight.shape[2], weight.shape[4]
    matrix = weight.reshape(3, 3, out_channels, 3 * in_channels)
    extra_in = -(3 * in_channels) % 16
    extra_out = -out_channels % 8
    return jnp.pad(matrix, ((0, 0), (0, 0), (0, extra_out), (0, extra_in)))


def convolve_flat(block, weight, out_rows):
    out = conv_flat(shifted_stack(block), kernel_matrix(weight), out_rows)
    return out[:, : weight.shape[2]]


def per_device(
    image_field,
    coil_maps,
    kspace_data,
    sampling_mask,
    consistency_weight,
    conv_first,
    conv_middle,
    conv_last,
):
    slab_rows = image_field.shape[1]
    coil_rows = image_field.shape[2]
    phases = coil_maps.shape[3]
    partitions = kspace_data.shape[2]
    pixels = image_field.astype(jnp.bfloat16)
    sensitivity = coil_maps.astype(jnp.float32)
    values = lax.all_gather(pixels, "coil", axis=2, tiled=True).astype(jnp.float32)[:, None]
    expanded = jnp.stack(
        [
            sensitivity[0] * values[0] - sensitivity[1] * values[1],
            sensitivity[0] * values[1] + sensitivity[1] * values[0],
        ]
    ).astype(jnp.bfloat16)
    spectrum = fourier_section(expanded, 4, False)
    spectrum = fourier_section(spectrum, 3, False)
    spectrum = lax.all_to_all(spectrum, "slab", split_axis=3, concat_axis=2, tiled=True)
    spectrum = fourier_section(spectrum, 2, False)
    weights_mask = sampling_mask.astype(jnp.float32)[None, None, :, :, None]
    residual = (
        weights_mask * (spectrum.astype(jnp.float32) - kspace_data.astype(jnp.float32))
    ).astype(jnp.bfloat16)
    residual = fourier_section(residual, 2, True)
    residual = lax.all_to_all(residual, "slab", split_axis=2, concat_axis=3, tiled=True)
    residual = fourier_section(residual, 3, True)
    restored = fourier_section(residual, 4, True).astype(jnp.float32)
    sensitivity = coil_maps.astype(jnp.float32)
    partial_value = jnp.stack(
        [
            jnp.sum(sensitivity[0] * restored[0] + sensitivity[1] * restored[1], axis=0),
            jnp.sum(sensitivity[0] * restored[1] - sensitivity[1] * restored[0], axis=0),
        ]
    )
    step_size = consistency_weight[0]
    coil_first = lax.axis_index("coil") * coil_rows
    slab_first = lax.axis_index("slab") * slab_rows
    weights = (conv_first, conv_middle, conv_last)
    scattered = lax.psum_scatter(
        (-step_size * partial_value).astype(jnp.bfloat16), "coil", scatter_dimension=2, tiled=True
    )
    updated = image_field + scattered.astype(jnp.float32)
    activations = padded_2(updated.astype(jnp.bfloat16), (("coil", 2),), 3)
    activations = padded_2(activations, (("slab", 1),), 3)
    depth, rows = activations.shape[1], activations.shape[2]
    activations = activations.transpose(1, 0, 2, 3).reshape(depth, 2, rows * READ)
    for layer_index, weight in enumerate(weights):
        rows = rows - 2
        output = convolve_flat(activations, weight, rows)
        if layer_index < 2:
            margin = 2 - layer_index
            depth_places = slab_first - margin + jnp.arange(output.shape[0], dtype=jnp.int32)
            row_places = coil_first - margin + jnp.arange(rows * READ, dtype=jnp.int32) // READ
            inside = (
                ((depth_places >= 0) & (depth_places < partitions))[:, None, None]
                & ((row_places >= 0) & (row_places < phases))[None, None, :]
            )
            activations = jnp.where(inside, jax.nn.relu(output), 0.0).astype(jnp.bfloat16)
    correction = output.reshape(slab_rows, 2, coil_rows, READ).transpose(1, 0, 2, 3)
    return updated + correction


def solution(mesh):
    placed = (
        P(None, "slab", "coil", None),
        P(None, "coil", "slab", None, None),
        P(None, "coil", None, "slab", None),
        P(None, "slab"),
        P(),
        P(),
        P(),
        P(),
    )
    return jax.shard_map(
        per_device,
        mesh=mesh,
        in_specs=placed,
        out_specs=P(None, "slab", "coil", None),
        check_vma=False,
    )
```

```python
import math

import jax
import jax.numpy as jnp
from jax import lax
from jax.experimental import pallas as pl
from jax.experimental.pallas import tpu as pltpu
from jax.sharding import PartitionSpec as P


def padded_2(block, sides, width):
    for axis, dim in sides:
        count = lax.axis_size(axis)
        forward = [(i, i + 1) for i in range(count - 1)]
        backward = [(target, source) for source, target in forward]
        low = lax.ppermute(
            lax.slice_in_dim(block, block.shape[dim] - width, None, axis=dim), axis, forward
        )
        high = lax.ppermute(lax.slice_in_dim(block, 0, width, axis=dim), axis, backward)
        block = jnp.concatenate([low, block, high], axis=dim)
    return block


def fourier_tables(length):
    points = jnp.arange(length, dtype=jnp.int32)
    product = points[:, None] * points[None, :] % length
    angles = product.astype(jnp.float32) * (2.0 * math.pi / length)
    scaling = 1.0 / math.sqrt(length)
    return jnp.stack([jnp.cos(angles) * scaling, jnp.sin(angles) * scaling]).astype(jnp.bfloat16)


def fourier_section(values, along, inverse):
    length = values.shape[along]
    tables = fourier_tables(length)
    cosine = tables[0]
    sine = -tables[1] if inverse else tables[1]
    matrix = jnp.stack([jnp.stack([cosine, sine], axis=1), jnp.stack([-sine, cosine], axis=1)])
    result = lax.dot_general(
        matrix, values, (((2, 3), (0, along)), ((), ())), preferred_element_type=jnp.float32
    )
    result = jnp.moveaxis(result, 1, along)
    return result.astype(jnp.bfloat16)


READ = 384
CHUNK = 1536

def conv_flat(stack, kernel, out_rows):
    depth_in, width, lanes_in = stack.shape
    out_depth = depth_in - 2
    out_channels = kernel.shape[2]
    lanes = out_rows * READ
    starts = range(0, lanes, CHUNK)

    def body(s0, s1, s2, w_ref, o_ref):
        sources = (s0, s1, s2)
        for start in starts:
            size = min(CHUNK, lanes - start)
            acc = jnp.zeros((out_channels, size), jnp.float32)
            for dz in range(3):
                for dy in range(3):
                    acc = acc + jnp.dot(
                        w_ref[dz, dy],
                        sources[dz][0, :, pl.ds(start + dy * READ, size)],
                        preferred_element_type=jnp.float32,
                    )
            o_ref[0, :, pl.ds(start, size)] = acc

    in_specs = [
        pl.BlockSpec((1, width, lanes_in), lambda z, dz=dz: (z + dz, 0, 0)) for dz in range(3)
    ] + [pl.BlockSpec(kernel.shape, lambda z: (0, 0, 0, 0))]
    return pl.pallas_call(
        body,
        grid=(out_depth,),
        in_specs=in_specs,
        out_specs=pl.BlockSpec((1, out_channels, lanes), lambda z: (z, 0, 0)),
        out_shape=jax.ShapeDtypeStruct((out_depth, out_channels, lanes), jnp.float32),
    )(stack, stack, stack, kernel)


def shifted_stack(block):
    channels = block.shape[1]
    left = jnp.pad(block, ((0, 0), (0, 0), (1, 0)))[..., :-1]
    right = jnp.pad(block, ((0, 0), (0, 0), (0, 1)))[..., 1:]
    place = lax.broadcasted_iota(jnp.int32, block.shape, 2) % READ
    zero = jnp.zeros((), block.dtype)
    left = jnp.where(place == 0, zero, left)
    right = jnp.where(place == READ - 1, zero, right)
    pieces = [left, block, right]
    extra = -(3 * channels) % 16
    if extra:
        pieces.append(jnp.zeros(block.shape[:1] + (extra,) + block.shape[2:], block.dtype))
    return jnp.concatenate(pieces, axis=1)


def kernel_matrix(weight):
    out_channels, in_channels = weight.shape[2], weight.shape[4]
    matrix = weight.reshape(3, 3, out_channels, 3 * in_channels)
    extra_in = -(3 * in_channels) % 16
    extra_out = -out_channels % 8
    return jnp.pad(matrix, ((0, 0), (0, 0), (0, extra_out), (0, extra_in)))


def convolve_flat(block, weight, out_rows):
    out = conv_flat(shifted_stack(block), kernel_matrix(weight), out_rows)
    return out[:, : weight.shape[2]]


def conv_roll(block, kernel, out_rows):
    depth_in, width, lanes_in = block.shape
    out_depth = depth_in - 2
    out_channels = kernel.shape[2] // 3
    lanes = out_rows * READ
    starts = range(0, lanes, CHUNK)

    def body(s0, s1, s2, w_ref, o_ref):
        sources = (s0, s1, s2)
        for start in starts:
            size = min(CHUNK, lanes - start)
            acc = jnp.zeros((3 * out_channels, size), jnp.float32)
            for dz in range(3):
                for dy in range(3):
                    acc = acc + jnp.dot(
                        w_ref[dz, dy],
                        sources[dz][0, :, pl.ds(start + dy * READ, size)],
                        preferred_element_type=jnp.float32,
                    )
            place = lax.broadcasted_iota(jnp.int32, (out_channels, size), 1) % READ
            left = pltpu.roll(acc[:out_channels], 1, 1)
            right = pltpu.roll(acc[2 * out_channels :], size - 1, 1)
            o_ref[0, :, pl.ds(start, size)] = (
                acc[out_channels : 2 * out_channels]
                + jnp.where(place == 0, 0.0, left)
                + jnp.where(place == READ - 1, 0.0, right)
            )

    in_specs = [
        pl.BlockSpec((1, width, lanes_in), lambda z, dz=dz: (z + dz, 0, 0)) for dz in range(3)
    ] + [pl.BlockSpec(kernel.shape, lambda z: (0, 0, 0, 0))]
    return pl.pallas_call(
        body,
        grid=(out_depth,),
        in_specs=in_specs,
        out_specs=pl.BlockSpec((1, out_channels, lanes), lambda z: (z, 0, 0)),
        out_shape=jax.ShapeDtypeStruct((out_depth, out_channels, lanes), jnp.float32),
    )(block, block, block, kernel)


def tap_matrix(weight):
    out_channels, in_channels = weight.shape[2], weight.shape[4]
    extra_out = -out_channels % 8
    extra_in = -in_channels % 16
    matrix = jnp.pad(
        weight.transpose(0, 1, 3, 2, 4), ((0, 0), (0, 0), (0, 0), (0, extra_out), (0, extra_in))
    )
    return matrix.reshape(3, 3, 3 * (out_channels + extra_out), in_channels + extra_in)


def padded_channels(block):
    extra = -block.shape[1] % 16
    if extra:
        block = jnp.pad(block, ((0, 0), (0, extra), (0, 0)))
    return block


def convolve_roll(block, weight, out_rows):
    out = conv_roll(padded_channels(block), tap_matrix(weight), out_rows)
    return out[:, : weight.shape[2]]


def per_device(
    image_field,
    coil_maps,
    kspace_data,
    sampling_mask,
    consistency_weight,
    conv_first,
    conv_middle,
    conv_last,
):
    slab_rows = image_field.shape[1]
    coil_rows = image_field.shape[2]
    phases = coil_maps.shape[3]
    partitions = kspace_data.shape[2]
    pixels = image_field.astype(jnp.bfloat16)
    sensitivity = coil_maps.astype(jnp.float32)
    values = lax.all_gather(pixels, "coil", axis=2, tiled=True).astype(jnp.float32)[:, None]
    expanded = jnp.stack(
        [
            sensitivity[0] * values[0] - sensitivity[1] * values[1],
            sensitivity[0] * values[1] + sensitivity[1] * values[0],
        ]
    ).astype(jnp.bfloat16)
    spectrum = fourier_section(expanded, 4, False)
    spectrum = fourier_section(spectrum, 3, False)
    spectrum = lax.all_to_all(spectrum, "slab", split_axis=3, concat_axis=2, tiled=True)
    spectrum = fourier_section(spectrum, 2, False)
    weights_mask = sampling_mask.astype(jnp.float32)[None, None, :, :, None]
    residual = (
        weights_mask * (spectrum.astype(jnp.float32) - kspace_data.astype(jnp.float32))
    ).astype(jnp.bfloat16)
    residual = fourier_section(residual, 2, True)
    residual = lax.all_to_all(residual, "slab", split_axis=2, concat_axis=3, tiled=True)
    residual = fourier_section(residual, 3, True)
    restored = fourier_section(residual, 4, True).astype(jnp.float32)
    sensitivity = coil_maps.astype(jnp.float32)
    partial_value = jnp.stack(
        [
            jnp.sum(sensitivity[0] * restored[0] + sensitivity[1] * restored[1], axis=0),
            jnp.sum(sensitivity[0] * restored[1] - sensitivity[1] * restored[0], axis=0),
        ]
    )
    step_size = consistency_weight[0]
    coil_first = lax.axis_index("coil") * coil_rows
    slab_first = lax.axis_index("slab") * slab_rows
    weights = (conv_first, conv_middle, conv_last)
    scattered = lax.psum_scatter(
        (-step_size * partial_value).astype(jnp.bfloat16), "coil", scatter_dimension=2, tiled=True
    )
    updated = image_field + scattered.astype(jnp.float32)
    activations = padded_2(updated.astype(jnp.bfloat16), (("coil", 2),), 3)
    activations = padded_2(activations, (("slab", 1),), 3)
    depth, rows = activations.shape[1], activations.shape[2]
    activations = activations.transpose(1, 0, 2, 3).reshape(depth, 2, rows * READ)
    for layer_index, weight in enumerate(weights):
        rows = rows - 2
        if layer_index == 0:
            output = convolve_flat(activations, weight, rows)
        else:
            output = convolve_roll(activations, weight, rows)
        if layer_index < 2:
            margin = 2 - layer_index
            depth_places = slab_first - margin + jnp.arange(output.shape[0], dtype=jnp.int32)
            row_places = coil_first - margin + jnp.arange(rows * READ, dtype=jnp.int32) // READ
            inside = (
                ((depth_places >= 0) & (depth_places < partitions))[:, None, None]
                & ((row_places >= 0) & (row_places < phases))[None, None, :]
            )
            activations = jnp.where(inside, jax.nn.relu(output), 0.0).astype(jnp.bfloat16)
    correction = output.reshape(slab_rows, 2, coil_rows, READ).transpose(1, 0, 2, 3)
    return updated + correction


def solution(mesh):
    placed = (
        P(None, "slab", "coil", None),
        P(None, "coil", "slab", None, None),
        P(None, "coil", None, "slab", None),
        P(None, "slab"),
        P(),
        P(),
        P(),
        P(),
    )
    return jax.shard_map(
        per_device,
        mesh=mesh,
        in_specs=placed,
        out_specs=P(None, "slab", "coil", None),
        check_vma=False,
    )
```

```python
import math

import jax
import jax.numpy as jnp
from jax import lax
from jax.experimental import pallas as pl
from jax.experimental.pallas import tpu as pltpu
from jax.sharding import PartitionSpec as P


def padded_2(block, sides, width):
    for axis, dim in sides:
        count = lax.axis_size(axis)
        forward = [(i, i + 1) for i in range(count - 1)]
        backward = [(target, source) for source, target in forward]
        low = lax.ppermute(
            lax.slice_in_dim(block, block.shape[dim] - width, None, axis=dim), axis, forward
        )
        high = lax.ppermute(lax.slice_in_dim(block, 0, width, axis=dim), axis, backward)
        block = jnp.concatenate([low, block, high], axis=dim)
    return block


def fourier_tables(length):
    points = jnp.arange(length, dtype=jnp.int32)
    product = points[:, None] * points[None, :] % length
    angles = product.astype(jnp.float32) * (2.0 * math.pi / length)
    scaling = 1.0 / math.sqrt(length)
    return jnp.stack([jnp.cos(angles) * scaling, jnp.sin(angles) * scaling]).astype(jnp.bfloat16)


def fourier_section(values, along, inverse):
    length = values.shape[along]
    tables = fourier_tables(length)
    cosine = tables[0]
    sine = -tables[1] if inverse else tables[1]
    matrix = jnp.stack([jnp.stack([cosine, sine], axis=1), jnp.stack([-sine, cosine], axis=1)])
    result = lax.dot_general(
        matrix, values, (((2, 3), (0, along)), ((), ())), preferred_element_type=jnp.float32
    )
    result = jnp.moveaxis(result, 1, along)
    return result.astype(jnp.bfloat16)


READ = 384
CHUNK = 1536

def finish(total, refs, start, size):
    if len(refs) == 1:
        return total
    keep = refs[0][0, :, pl.ds(start, size)] > 0
    return jnp.where(keep, jnp.maximum(total, 0.0), 0.0).astype(jnp.bfloat16)


def conv_flat(stack, kernel, out_rows, inside=None):
    depth_in, width, lanes_in = stack.shape
    out_depth = depth_in - 2
    out_channels = kernel.shape[2]
    lanes = out_rows * READ
    starts = range(0, lanes, CHUNK)

    def body(s0, s1, s2, w_ref, *refs):
        o_ref = refs[-1]
        sources = (s0, s1, s2)
        for start in starts:
            size = min(CHUNK, lanes - start)
            acc = jnp.zeros((out_channels, size), jnp.float32)
            for dz in range(3):
                for dy in range(3):
                    acc = acc + jnp.dot(
                        w_ref[dz, dy],
                        sources[dz][0, :, pl.ds(start + dy * READ, size)],
                        preferred_element_type=jnp.float32,
                    )
            o_ref[0, :, pl.ds(start, size)] = finish(acc, refs, start, size)

    in_specs = [
        pl.BlockSpec((1, width, lanes_in), lambda z, dz=dz: (z + dz, 0, 0)) for dz in range(3)
    ] + [pl.BlockSpec(kernel.shape, lambda z: (0, 0, 0, 0))]
    extra = ()
    kind = jnp.float32
    if inside is not None:
        in_specs.append(pl.BlockSpec((1, 1, lanes), lambda z: (z, 0, 0)))
        extra = (inside,)
        kind = jnp.bfloat16
    return pl.pallas_call(
        body,
        grid=(out_depth,),
        in_specs=in_specs,
        out_specs=pl.BlockSpec((1, out_channels, lanes), lambda z: (z, 0, 0)),
        out_shape=jax.ShapeDtypeStruct((out_depth, out_channels, lanes), kind),
    )(stack, stack, stack, kernel, *extra)


def shifted_stack(block):
    channels = block.shape[1]
    left = jnp.pad(block, ((0, 0), (0, 0), (1, 0)))[..., :-1]
    right = jnp.pad(block, ((0, 0), (0, 0), (0, 1)))[..., 1:]
    place = lax.broadcasted_iota(jnp.int32, block.shape, 2) % READ
    zero = jnp.zeros((), block.dtype)
    left = jnp.where(place == 0, zero, left)
    right = jnp.where(place == READ - 1, zero, right)
    pieces = [left, block, right]
    extra = -(3 * channels) % 16
    if extra:
        pieces.append(jnp.zeros(block.shape[:1] + (extra,) + block.shape[2:], block.dtype))
    return jnp.concatenate(pieces, axis=1)


def kernel_matrix(weight):
    out_channels, in_channels = weight.shape[2], weight.shape[4]
    matrix = weight.reshape(3, 3, out_channels, 3 * in_channels)
    extra_in = -(3 * in_channels) % 16
    extra_out = -out_channels % 8
    return jnp.pad(matrix, ((0, 0), (0, 0), (0, extra_out), (0, extra_in)))


def convolve_flat(block, weight, out_rows, inside=None):
    out = conv_flat(shifted_stack(block), kernel_matrix(weight), out_rows, inside)
    return out[:, : weight.shape[2]]


def conv_roll(block, kernel, out_rows, inside=None):
    depth_in, width, lanes_in = block.shape
    out_depth = depth_in - 2
    out_channels = kernel.shape[2] // 3
    lanes = out_rows * READ
    starts = range(0, lanes, CHUNK)

    def body(s0, s1, s2, w_ref, *refs):
        o_ref = refs[-1]
        sources = (s0, s1, s2)
        for start in starts:
            size = min(CHUNK, lanes - start)
            acc = jnp.zeros((3 * out_channels, size), jnp.float32)
            for dz in range(3):
                for dy in range(3):
                    acc = acc + jnp.dot(
                        w_ref[dz, dy],
                        sources[dz][0, :, pl.ds(start + dy * READ, size)],
                        preferred_element_type=jnp.float32,
                    )
            place = lax.broadcasted_iota(jnp.int32, (out_channels, size), 1) % READ
            left = pltpu.roll(acc[:out_channels], 1, 1)
            right = pltpu.roll(acc[2 * out_channels :], size - 1, 1)
            total = (
                acc[out_channels : 2 * out_channels]
                + jnp.where(place == 0, 0.0, left)
                + jnp.where(place == READ - 1, 0.0, right)
            )
            o_ref[0, :, pl.ds(start, size)] = finish(total, refs, start, size)

    in_specs = [
        pl.BlockSpec((1, width, lanes_in), lambda z, dz=dz: (z + dz, 0, 0)) for dz in range(3)
    ] + [pl.BlockSpec(kernel.shape, lambda z: (0, 0, 0, 0))]
    extra = ()
    kind = jnp.float32
    if inside is not None:
        in_specs.append(pl.BlockSpec((1, 1, lanes), lambda z: (z, 0, 0)))
        extra = (inside,)
        kind = jnp.bfloat16
    return pl.pallas_call(
        body,
        grid=(out_depth,),
        in_specs=in_specs,
        out_specs=pl.BlockSpec((1, out_channels, lanes), lambda z: (z, 0, 0)),
        out_shape=jax.ShapeDtypeStruct((out_depth, out_channels, lanes), kind),
    )(block, block, block, kernel, *extra)


def tap_matrix(weight):
    out_channels, in_channels = weight.shape[2], weight.shape[4]
    extra_out = -out_channels % 8
    extra_in = -in_channels % 16
    matrix = jnp.pad(
        weight.transpose(0, 1, 3, 2, 4), ((0, 0), (0, 0), (0, 0), (0, extra_out), (0, extra_in))
    )
    return matrix.reshape(3, 3, 3 * (out_channels + extra_out), in_channels + extra_in)


def padded_channels(block):
    extra = -block.shape[1] % 16
    if extra:
        block = jnp.pad(block, ((0, 0), (0, extra), (0, 0)))
    return block


def convolve_roll(block, weight, out_rows, inside=None):
    out = conv_roll(padded_channels(block), tap_matrix(weight), out_rows, inside)
    return out[:, : weight.shape[2]]


def per_device(
    image_field,
    coil_maps,
    kspace_data,
    sampling_mask,
    consistency_weight,
    conv_first,
    conv_middle,
    conv_last,
):
    slab_rows = image_field.shape[1]
    coil_rows = image_field.shape[2]
    phases = coil_maps.shape[3]
    partitions = kspace_data.shape[2]
    pixels = image_field.astype(jnp.bfloat16)
    sensitivity = coil_maps.astype(jnp.float32)
    values = lax.all_gather(pixels, "coil", axis=2, tiled=True).astype(jnp.float32)[:, None]
    expanded = jnp.stack(
        [
            sensitivity[0] * values[0] - sensitivity[1] * values[1],
            sensitivity[0] * values[1] + sensitivity[1] * values[0],
        ]
    ).astype(jnp.bfloat16)
    spectrum = fourier_section(expanded, 4, False)
    spectrum = fourier_section(spectrum, 3, False)
    spectrum = lax.all_to_all(spectrum, "slab", split_axis=3, concat_axis=2, tiled=True)
    spectrum = fourier_section(spectrum, 2, False)
    weights_mask = sampling_mask.astype(jnp.float32)[None, None, :, :, None]
    residual = (
        weights_mask * (spectrum.astype(jnp.float32) - kspace_data.astype(jnp.float32))
    ).astype(jnp.bfloat16)
    residual = fourier_section(residual, 2, True)
    residual = lax.all_to_all(residual, "slab", split_axis=2, concat_axis=3, tiled=True)
    residual = fourier_section(residual, 3, True)
    restored = fourier_section(residual, 4, True).astype(jnp.float32)
    sensitivity = coil_maps.astype(jnp.float32)
    partial_value = jnp.stack(
        [
            jnp.sum(sensitivity[0] * restored[0] + sensitivity[1] * restored[1], axis=0),
            jnp.sum(sensitivity[0] * restored[1] - sensitivity[1] * restored[0], axis=0),
        ]
    )
    step_size = consistency_weight[0]
    coil_first = lax.axis_index("coil") * coil_rows
    slab_first = lax.axis_index("slab") * slab_rows
    weights = (conv_first, conv_middle, conv_last)
    scattered = lax.psum_scatter(
        (-step_size * partial_value).astype(jnp.bfloat16), "coil", scatter_dimension=2, tiled=True
    )
    updated = image_field + scattered.astype(jnp.float32)
    activations = padded_2(updated.astype(jnp.bfloat16), (("coil", 2),), 3)
    activations = padded_2(activations, (("slab", 1),), 3)
    depth, rows = activations.shape[1], activations.shape[2]
    activations = activations.transpose(1, 0, 2, 3).reshape(depth, 2, rows * READ)
    for layer_index, weight in enumerate(weights):
        rows = rows - 2
        inside = None
        if layer_index < 2:
            margin = 2 - layer_index
            depth_places = slab_first - margin + jnp.arange(depth - 2, dtype=jnp.int32)
            row_places = coil_first - margin + jnp.arange(rows * READ, dtype=jnp.int32) // READ
            inside = (
                ((depth_places >= 0) & (depth_places < partitions))[:, None, None]
                & ((row_places >= 0) & (row_places < phases))[None, None, :]
            ).astype(jnp.float32)
        depth = depth - 2
        if layer_index == 0:
            output = convolve_flat(activations, weight, rows, inside)
        else:
            output = convolve_roll(activations, weight, rows, inside)
        activations = output
    correction = output.reshape(slab_rows, 2, coil_rows, READ).transpose(1, 0, 2, 3)
    return updated + correction


def solution(mesh):
    placed = (
        P(None, "slab", "coil", None),
        P(None, "coil", "slab", None, None),
        P(None, "coil", None, "slab", None),
        P(None, "slab"),
        P(),
        P(),
        P(),
        P(),
    )
    return jax.shard_map(
        per_device,
        mesh=mesh,
        in_specs=placed,
        out_specs=P(None, "slab", "coil", None),
        check_vma=False,
    )
```

```python
import math

import jax
import jax.numpy as jnp
from jax import lax
from jax.experimental import pallas as pl
from jax.experimental.pallas import tpu as pltpu
from jax.sharding import PartitionSpec as P


def padded_2(block, sides, width):
    for axis, dim in sides:
        count = lax.axis_size(axis)
        forward = [(i, i + 1) for i in range(count - 1)]
        backward = [(target, source) for source, target in forward]
        low = lax.ppermute(
            lax.slice_in_dim(block, block.shape[dim] - width, None, axis=dim), axis, forward
        )
        high = lax.ppermute(lax.slice_in_dim(block, 0, width, axis=dim), axis, backward)
        block = jnp.concatenate([low, block, high], axis=dim)
    return block


def fourier_tables(length):
    points = jnp.arange(length, dtype=jnp.int32)
    product = points[:, None] * points[None, :] % length
    angles = product.astype(jnp.float32) * (2.0 * math.pi / length)
    scaling = 1.0 / math.sqrt(length)
    return jnp.stack([jnp.cos(angles) * scaling, jnp.sin(angles) * scaling]).astype(jnp.bfloat16)


def fourier_section(values, along, inverse):
    length = values.shape[along]
    tables = fourier_tables(length)
    cosine = tables[0]
    sine = -tables[1] if inverse else tables[1]
    matrix = jnp.stack([jnp.stack([cosine, sine], axis=1), jnp.stack([-sine, cosine], axis=1)])
    result = lax.dot_general(
        matrix, values, (((2, 3), (0, along)), ((), ())), preferred_element_type=jnp.float32
    )
    result = jnp.moveaxis(result, 1, along)
    return result.astype(jnp.bfloat16)


READ = 384
CHUNK = 1536

def finish(total, refs, start, size):
    if len(refs) == 1:
        return total
    keep = refs[0][0, :, pl.ds(start, size)] > 0
    return jnp.where(keep, jnp.maximum(total, 0.0), 0.0).astype(jnp.bfloat16)


def conv_flat(stack, kernel, out_rows, inside=None):
    depth_in, width, lanes_in = stack.shape
    out_depth = depth_in - 2
    out_channels = kernel.shape[2]
    lanes = out_rows * READ
    starts = range(0, lanes, CHUNK)

    def body(s0, s1, s2, w_ref, *refs):
        o_ref = refs[-1]
        sources = (s0, s1, s2)
        for start in starts:
            size = min(CHUNK, lanes - start)
            acc = jnp.zeros((out_channels, size), jnp.float32)
            for dz in range(3):
                for dy in range(3):
                    acc = acc + jnp.dot(
                        w_ref[dz, dy],
                        sources[dz][0, :, pl.ds(start + dy * READ, size)],
                        preferred_element_type=jnp.float32,
                    )
            o_ref[0, :, pl.ds(start, size)] = finish(acc, refs, start, size)

    in_specs = [
        pl.BlockSpec((1, width, lanes_in), lambda z, dz=dz: (z + dz, 0, 0)) for dz in range(3)
    ] + [pl.BlockSpec(kernel.shape, lambda z: (0, 0, 0, 0))]
    extra = ()
    kind = jnp.float32
    if inside is not None:
        in_specs.append(pl.BlockSpec((1, 1, lanes), lambda z: (z, 0, 0)))
        extra = (inside,)
        kind = jnp.bfloat16
    return pl.pallas_call(
        body,
        grid=(out_depth,),
        in_specs=in_specs,
        out_specs=pl.BlockSpec((1, out_channels, lanes), lambda z: (z, 0, 0)),
        out_shape=jax.ShapeDtypeStruct((out_depth, out_channels, lanes), kind),
    )(stack, stack, stack, kernel, *extra)


def shifted_stack(block):
    channels = block.shape[1]
    left = jnp.pad(block, ((0, 0), (0, 0), (1, 0)))[..., :-1]
    right = jnp.pad(block, ((0, 0), (0, 0), (0, 1)))[..., 1:]
    place = lax.broadcasted_iota(jnp.int32, block.shape, 2) % READ
    zero = jnp.zeros((), block.dtype)
    left = jnp.where(place == 0, zero, left)
    right = jnp.where(place == READ - 1, zero, right)
    pieces = [left, block, right]
    extra = -(3 * channels) % 16
    if extra:
        pieces.append(jnp.zeros(block.shape[:1] + (extra,) + block.shape[2:], block.dtype))
    return jnp.concatenate(pieces, axis=1)


def kernel_matrix(weight):
    out_channels, in_channels = weight.shape[2], weight.shape[4]
    matrix = weight.reshape(3, 3, out_channels, 3 * in_channels)
    extra_in = -(3 * in_channels) % 16
    extra_out = -out_channels % 8
    return jnp.pad(matrix, ((0, 0), (0, 0), (0, extra_out), (0, extra_in)))


def convolve_flat(block, weight, out_rows, inside=None):
    out = conv_flat(shifted_stack(block), kernel_matrix(weight), out_rows, inside)
    return out[:, : weight.shape[2]]


def conv_roll(block, kernel, out_rows, inside=None):
    depth_in, width, lanes_in = block.shape
    out_depth = depth_in - 2
    out_channels = kernel.shape[2] // 3
    lanes = out_rows * READ
    starts = range(0, lanes, CHUNK)

    def body(s0, s1, s2, w_ref, *refs):
        o_ref = refs[-1]
        sources = (s0, s1, s2)
        for start in starts:
            size = min(CHUNK, lanes - start)
            acc = jnp.zeros((3 * out_channels, size), jnp.float32)
            for dz in range(3):
                for dy in range(3):
                    acc = acc + jnp.dot(
                        w_ref[dz, dy],
                        sources[dz][0, :, pl.ds(start + dy * READ, size)],
                        preferred_element_type=jnp.float32,
                    )
            place = lax.broadcasted_iota(jnp.int32, (out_channels, size), 1) % READ
            left = pltpu.roll(acc[:out_channels], 1, 1)
            right = pltpu.roll(acc[2 * out_channels :], size - 1, 1)
            total = (
                acc[out_channels : 2 * out_channels]
                + jnp.where(place == 0, 0.0, left)
                + jnp.where(place == READ - 1, 0.0, right)
            )
            o_ref[0, :, pl.ds(start, size)] = finish(total, refs, start, size)

    in_specs = [
        pl.BlockSpec((1, width, lanes_in), lambda z, dz=dz: (z + dz, 0, 0)) for dz in range(3)
    ] + [pl.BlockSpec(kernel.shape, lambda z: (0, 0, 0, 0))]
    extra = ()
    kind = jnp.float32
    if inside is not None:
        in_specs.append(pl.BlockSpec((1, 1, lanes), lambda z: (z, 0, 0)))
        extra = (inside,)
        kind = jnp.bfloat16
    return pl.pallas_call(
        body,
        grid=(out_depth,),
        in_specs=in_specs,
        out_specs=pl.BlockSpec((1, out_channels, lanes), lambda z: (z, 0, 0)),
        out_shape=jax.ShapeDtypeStruct((out_depth, out_channels, lanes), kind),
    )(block, block, block, kernel, *extra)


def tap_matrix(weight):
    out_channels, in_channels = weight.shape[2], weight.shape[4]
    extra_out = -out_channels % 8
    extra_in = -in_channels % 16
    matrix = jnp.pad(
        weight.transpose(0, 1, 3, 2, 4), ((0, 0), (0, 0), (0, 0), (0, extra_out), (0, extra_in))
    )
    return matrix.reshape(3, 3, 3 * (out_channels + extra_out), in_channels + extra_in)


def padded_channels(block):
    extra = -block.shape[1] % 16
    if extra:
        block = jnp.pad(block, ((0, 0), (0, extra), (0, 0)))
    return block


def convolve_roll(block, weight, out_rows, inside=None):
    out = conv_roll(padded_channels(block), tap_matrix(weight), out_rows, inside)
    return out[:, : weight.shape[2]]


def per_device(
    image_field,
    coil_maps,
    kspace_data,
    sampling_mask,
    consistency_weight,
    conv_first,
    conv_middle,
    conv_last,
):
    slab_rows = image_field.shape[1]
    coil_rows = image_field.shape[2]
    phases = coil_maps.shape[3]
    partitions = kspace_data.shape[2]
    pixels = image_field.astype(jnp.bfloat16)
    sensitivity = coil_maps.astype(jnp.float32)
    values = lax.all_gather(pixels, "coil", axis=2, tiled=True).astype(jnp.float32)[:, None]
    expanded = jnp.stack(
        [
            sensitivity[0] * values[0] - sensitivity[1] * values[1],
            sensitivity[0] * values[1] + sensitivity[1] * values[0],
        ]
    ).astype(jnp.bfloat16)
    spectrum = fourier_section(expanded, 4, False)
    spectrum = fourier_section(spectrum, 3, False)
    spectrum = lax.all_to_all(spectrum, "slab", split_axis=3, concat_axis=2, tiled=True)
    spectrum = fourier_section(spectrum, 2, False)
    weights_mask = sampling_mask.astype(jnp.float32)[None, None, :, :, None]
    residual = (
        weights_mask * (spectrum.astype(jnp.float32) - kspace_data.astype(jnp.float32))
    ).astype(jnp.bfloat16)
    residual = fourier_section(residual, 2, True)
    residual = lax.all_to_all(residual, "slab", split_axis=2, concat_axis=3, tiled=True)
    step_size = consistency_weight[0]
    coil_first = lax.axis_index("coil") * coil_rows
    slab_first = lax.axis_index("slab") * slab_rows
    weights = (conv_first, conv_middle, conv_last)
    half = slab_rows // 2
    pieces = []
    for first in (0, half):
        part = lax.slice_in_dim(residual, first, first + half, axis=2)
        part = fourier_section(part, 3, True)
        restored = fourier_section(part, 4, True).astype(jnp.float32)
        sensitivity = lax.slice_in_dim(coil_maps, first, first + half, axis=2).astype(jnp.float32)
        partial_value = jnp.stack(
            [
                jnp.sum(sensitivity[0] * restored[0] + sensitivity[1] * restored[1], axis=0),
                jnp.sum(sensitivity[0] * restored[1] - sensitivity[1] * restored[0], axis=0),
            ]
        )
        pieces.append(
            lax.psum_scatter(
                (-step_size * partial_value).astype(jnp.bfloat16),
                "coil",
                scatter_dimension=2,
                tiled=True,
            )
        )
    scattered = jnp.concatenate(pieces, axis=1)
    updated = image_field + scattered.astype(jnp.float32)
    activations = padded_2(updated.astype(jnp.bfloat16), (("coil", 2),), 3)
    activations = padded_2(activations, (("slab", 1),), 3)
    depth, rows = activations.shape[1], activations.shape[2]
    activations = activations.transpose(1, 0, 2, 3).reshape(depth, 2, rows * READ)
    for layer_index, weight in enumerate(weights):
        rows = rows - 2
        inside = None
        if layer_index < 2:
            margin = 2 - layer_index
            depth_places = slab_first - margin + jnp.arange(depth - 2, dtype=jnp.int32)
            row_places = coil_first - margin + jnp.arange(rows * READ, dtype=jnp.int32) // READ
            inside = (
                ((depth_places >= 0) & (depth_places < partitions))[:, None, None]
                & ((row_places >= 0) & (row_places < phases))[None, None, :]
            ).astype(jnp.float32)
        depth = depth - 2
        if layer_index == 0:
            output = convolve_flat(activations, weight, rows, inside)
        else:
            output = convolve_roll(activations, weight, rows, inside)
        activations = output
    correction = output.reshape(slab_rows, 2, coil_rows, READ).transpose(1, 0, 2, 3)
    return updated + correction


def solution(mesh):
    placed = (
        P(None, "slab", "coil", None),
        P(None, "coil", "slab", None, None),
        P(None, "coil", None, "slab", None),
        P(None, "slab"),
        P(),
        P(),
        P(),
        P(),
    )
    return jax.shard_map(
        per_device,
        mesh=mesh,
        in_specs=placed,
        out_specs=P(None, "slab", "coil", None),
        check_vma=False,
    )
```

```python
import math

import jax
import jax.numpy as jnp
from jax import lax
from jax.experimental import pallas as pl
from jax.experimental.pallas import tpu as pltpu
from jax.sharding import PartitionSpec as P


def padded_2(block, sides, width):
    for axis, dim in sides:
        count = lax.axis_size(axis)
        forward = [(i, i + 1) for i in range(count - 1)]
        backward = [(target, source) for source, target in forward]
        low = lax.ppermute(
            lax.slice_in_dim(block, block.shape[dim] - width, None, axis=dim), axis, forward
        )
        high = lax.ppermute(lax.slice_in_dim(block, 0, width, axis=dim), axis, backward)
        block = jnp.concatenate([low, block, high], axis=dim)
    return block


def fourier_tables(length):
    points = jnp.arange(length, dtype=jnp.int32)
    product = points[:, None] * points[None, :] % length
    angles = product.astype(jnp.float32) * (2.0 * math.pi / length)
    scaling = 1.0 / math.sqrt(length)
    return jnp.stack([jnp.cos(angles) * scaling, jnp.sin(angles) * scaling]).astype(jnp.bfloat16)


def fourier_section(values, along, inverse):
    length = values.shape[along]
    tables = fourier_tables(length)
    cosine = tables[0]
    sine = -tables[1] if inverse else tables[1]
    matrix = jnp.stack([jnp.stack([cosine, sine], axis=1), jnp.stack([-sine, cosine], axis=1)])
    result = lax.dot_general(
        matrix, values, (((2, 3), (0, along)), ((), ())), preferred_element_type=jnp.float32
    )
    result = jnp.moveaxis(result, 1, along)
    return result.astype(jnp.bfloat16)


READ = 384
CHUNK = 1536

def finish(total, refs, start, size):
    if len(refs) == 1:
        return total
    keep = refs[0][0, :, pl.ds(start, size)] > 0
    return jnp.where(keep, jnp.maximum(total, 0.0), 0.0).astype(jnp.bfloat16)


def conv_flat(stack, kernel, out_rows, inside=None):
    depth_in, width, lanes_in = stack.shape
    out_depth = depth_in - 2
    out_channels = kernel.shape[2]
    lanes = out_rows * READ
    starts = range(0, lanes, CHUNK)

    def body(s0, s1, s2, w_ref, *refs):
        o_ref = refs[-1]
        sources = (s0, s1, s2)
        for start in starts:
            size = min(CHUNK, lanes - start)
            acc = jnp.zeros((out_channels, size), jnp.float32)
            for dz in range(3):
                for dy in range(3):
                    acc = acc + jnp.dot(
                        w_ref[dz, dy],
                        sources[dz][0, :, pl.ds(start + dy * READ, size)],
                        preferred_element_type=jnp.float32,
                    )
            o_ref[0, :, pl.ds(start, size)] = finish(acc, refs, start, size)

    in_specs = [
        pl.BlockSpec((1, width, lanes_in), lambda z, dz=dz: (z + dz, 0, 0)) for dz in range(3)
    ] + [pl.BlockSpec(kernel.shape, lambda z: (0, 0, 0, 0))]
    extra = ()
    kind = jnp.float32
    if inside is not None:
        in_specs.append(pl.BlockSpec((1, 1, lanes), lambda z: (z, 0, 0)))
        extra = (inside,)
        kind = jnp.bfloat16
    return pl.pallas_call(
        body,
        grid=(out_depth,),
        in_specs=in_specs,
        out_specs=pl.BlockSpec((1, out_channels, lanes), lambda z: (z, 0, 0)),
        out_shape=jax.ShapeDtypeStruct((out_depth, out_channels, lanes), kind),
    )(stack, stack, stack, kernel, *extra)


def shifted_stack(block):
    channels = block.shape[1]
    left = jnp.pad(block, ((0, 0), (0, 0), (1, 0)))[..., :-1]
    right = jnp.pad(block, ((0, 0), (0, 0), (0, 1)))[..., 1:]
    place = lax.broadcasted_iota(jnp.int32, block.shape, 2) % READ
    zero = jnp.zeros((), block.dtype)
    left = jnp.where(place == 0, zero, left)
    right = jnp.where(place == READ - 1, zero, right)
    pieces = [left, block, right]
    extra = -(3 * channels) % 16
    if extra:
        pieces.append(jnp.zeros(block.shape[:1] + (extra,) + block.shape[2:], block.dtype))
    return jnp.concatenate(pieces, axis=1)


def kernel_matrix(weight):
    out_channels, in_channels = weight.shape[2], weight.shape[4]
    matrix = weight.reshape(3, 3, out_channels, 3 * in_channels)
    extra_in = -(3 * in_channels) % 16
    extra_out = -out_channels % 8
    return jnp.pad(matrix, ((0, 0), (0, 0), (0, extra_out), (0, extra_in)))


def convolve_flat(block, weight, out_rows, inside=None):
    out = conv_flat(shifted_stack(block), kernel_matrix(weight), out_rows, inside)
    return out[:, : weight.shape[2]]


def conv_roll(block, kernel, out_rows, inside=None):
    depth_in, width, lanes_in = block.shape
    out_depth = depth_in - 2
    out_channels = kernel.shape[2] // 3
    lanes = out_rows * READ
    starts = range(0, lanes, CHUNK)

    def body(s0, s1, s2, w_ref, *refs):
        o_ref = refs[-1]
        sources = (s0, s1, s2)
        for start in starts:
            size = min(CHUNK, lanes - start)
            acc = jnp.zeros((3 * out_channels, size), jnp.float32)
            for dz in range(3):
                for dy in range(3):
                    acc = acc + jnp.dot(
                        w_ref[dz, dy],
                        sources[dz][0, :, pl.ds(start + dy * READ, size)],
                        preferred_element_type=jnp.float32,
                    )
            place = lax.broadcasted_iota(jnp.int32, (out_channels, size), 1) % READ
            left = pltpu.roll(acc[:out_channels], 1, 1)
            right = pltpu.roll(acc[2 * out_channels :], size - 1, 1)
            total = (
                acc[out_channels : 2 * out_channels]
                + jnp.where(place == 0, 0.0, left)
                + jnp.where(place == READ - 1, 0.0, right)
            )
            o_ref[0, :, pl.ds(start, size)] = finish(total, refs, start, size)

    in_specs = [
        pl.BlockSpec((1, width, lanes_in), lambda z, dz=dz: (z + dz, 0, 0)) for dz in range(3)
    ] + [pl.BlockSpec(kernel.shape, lambda z: (0, 0, 0, 0))]
    extra = ()
    kind = jnp.float32
    if inside is not None:
        in_specs.append(pl.BlockSpec((1, 1, lanes), lambda z: (z, 0, 0)))
        extra = (inside,)
        kind = jnp.bfloat16
    return pl.pallas_call(
        body,
        grid=(out_depth,),
        in_specs=in_specs,
        out_specs=pl.BlockSpec((1, out_channels, lanes), lambda z: (z, 0, 0)),
        out_shape=jax.ShapeDtypeStruct((out_depth, out_channels, lanes), kind),
    )(block, block, block, kernel, *extra)


def tap_matrix(weight):
    out_channels, in_channels = weight.shape[2], weight.shape[4]
    extra_out = -out_channels % 8
    extra_in = -in_channels % 16
    matrix = jnp.pad(
        weight.transpose(0, 1, 3, 2, 4), ((0, 0), (0, 0), (0, 0), (0, extra_out), (0, extra_in))
    )
    return matrix.reshape(3, 3, 3 * (out_channels + extra_out), in_channels + extra_in)


def padded_channels(block):
    extra = -block.shape[1] % 16
    if extra:
        block = jnp.pad(block, ((0, 0), (0, extra), (0, 0)))
    return block


def convolve_roll(block, weight, out_rows, inside=None):
    out = conv_roll(padded_channels(block), tap_matrix(weight), out_rows, inside)
    return out[:, : weight.shape[2]]


def per_device(
    image_field,
    coil_maps,
    kspace_data,
    sampling_mask,
    consistency_weight,
    conv_first,
    conv_middle,
    conv_last,
):
    slab_rows = image_field.shape[1]
    coil_rows = image_field.shape[2]
    phases = coil_maps.shape[3]
    partitions = kspace_data.shape[2]
    pixels = image_field.astype(jnp.bfloat16)
    sensitivity = coil_maps.astype(jnp.float32)
    values = lax.all_gather(pixels, "coil", axis=2, tiled=True).astype(jnp.float32)[:, None]
    expanded = jnp.stack(
        [
            sensitivity[0] * values[0] - sensitivity[1] * values[1],
            sensitivity[0] * values[1] + sensitivity[1] * values[0],
        ]
    ).astype(jnp.bfloat16)
    spectrum = fourier_section(expanded, 4, False)
    spectrum = fourier_section(spectrum, 3, False)
    spectrum = lax.all_to_all(spectrum, "slab", split_axis=3, concat_axis=2, tiled=True)
    spectrum = fourier_section(spectrum, 2, False)
    weights_mask = sampling_mask.astype(jnp.float32)[None, None, :, :, None]
    residual = (
        weights_mask * (spectrum.astype(jnp.float32) - kspace_data.astype(jnp.float32))
    ).astype(jnp.bfloat16)
    residual = fourier_section(residual, 2, True)
    residual = lax.all_to_all(residual, "slab", split_axis=2, concat_axis=3, tiled=True)
    residual = fourier_section(residual, 3, True)
    restored = fourier_section(residual, 4, True).astype(jnp.float32)
    sensitivity = coil_maps.astype(jnp.float32)
    partial_value = jnp.stack(
        [
            jnp.sum(sensitivity[0] * restored[0] + sensitivity[1] * restored[1], axis=0),
            jnp.sum(sensitivity[0] * restored[1] - sensitivity[1] * restored[0], axis=0),
        ]
    )
    step_size = consistency_weight[0]
    coil_first = lax.axis_index("coil") * coil_rows
    slab_first = lax.axis_index("slab") * slab_rows
    weights = (conv_first, conv_middle, conv_last)
    gathered = lax.all_to_all(
        (-step_size * partial_value).astype(jnp.bfloat16), "coil", 2, 2, tiled=True
    )
    coils = lax.axis_size("coil")
    scattered = jnp.sum(
        gathered.astype(jnp.float32).reshape(2, slab_rows, coils, coil_rows, READ), axis=2
    )
    updated = image_field + scattered
    activations = padded_2(updated.astype(jnp.bfloat16), (("coil", 2),), 3)
    activations = padded_2(activations, (("slab", 1),), 3)
    depth, rows = activations.shape[1], activations.shape[2]
    activations = activations.transpose(1, 0, 2, 3).reshape(depth, 2, rows * READ)
    for layer_index, weight in enumerate(weights):
        rows = rows - 2
        inside = None
        if layer_index < 2:
            margin = 2 - layer_index
            depth_places = slab_first - margin + jnp.arange(depth - 2, dtype=jnp.int32)
            row_places = coil_first - margin + jnp.arange(rows * READ, dtype=jnp.int32) // READ
            inside = (
                ((depth_places >= 0) & (depth_places < partitions))[:, None, None]
                & ((row_places >= 0) & (row_places < phases))[None, None, :]
            ).astype(jnp.float32)
        depth = depth - 2
        if layer_index == 0:
            output = convolve_flat(activations, weight, rows, inside)
        else:
            output = convolve_roll(activations, weight, rows, inside)
        activations = output
    correction = output.reshape(slab_rows, 2, coil_rows, READ).transpose(1, 0, 2, 3)
    return updated + correction


def solution(mesh):
    placed = (
        P(None, "slab", "coil", None),
        P(None, "coil", "slab", None, None),
        P(None, "coil", None, "slab", None),
        P(None, "slab"),
        P(),
        P(),
        P(),
        P(),
    )
    return jax.shard_map(
        per_device,
        mesh=mesh,
        in_specs=placed,
        out_specs=P(None, "slab", "coil", None),
        check_vma=False,
    )
```

```python
import math

import jax
import jax.numpy as jnp
from jax import lax
from jax.experimental import pallas as pl
from jax.experimental.pallas import tpu as pltpu
from jax.sharding import PartitionSpec as P


def padded_2(block, sides, width):
    for axis, dim in sides:
        count = lax.axis_size(axis)
        forward = [(i, i + 1) for i in range(count - 1)]
        backward = [(target, source) for source, target in forward]
        low = lax.ppermute(
            lax.slice_in_dim(block, block.shape[dim] - width, None, axis=dim), axis, forward
        )
        high = lax.ppermute(lax.slice_in_dim(block, 0, width, axis=dim), axis, backward)
        block = jnp.concatenate([low, block, high], axis=dim)
    return block


def fourier_tables(length):
    points = jnp.arange(length, dtype=jnp.int32)
    product = points[:, None] * points[None, :] % length
    angles = product.astype(jnp.float32) * (2.0 * math.pi / length)
    scaling = 1.0 / math.sqrt(length)
    return jnp.stack([jnp.cos(angles) * scaling, jnp.sin(angles) * scaling]).astype(jnp.bfloat16)


def fourier_section(values, along, inverse):
    length = values.shape[along]
    tables = fourier_tables(length)
    cosine = tables[0]
    sine = -tables[1] if inverse else tables[1]
    matrix = jnp.stack([jnp.stack([cosine, sine], axis=1), jnp.stack([-sine, cosine], axis=1)])
    result = lax.dot_general(
        matrix, values, (((2, 3), (0, along)), ((), ())), preferred_element_type=jnp.float32
    )
    result = jnp.moveaxis(result, 1, along)
    return result.astype(jnp.bfloat16)


READ = 384
CHUNK = 1536

def finish(total, refs, start, size, spread):
    if len(refs) == 1:
        return total
    keep = refs[0][0, :, pl.ds(start, size)] > 0
    kept = jnp.where(keep, jnp.maximum(total, 0.0), 0.0)
    if not spread:
        return kept.astype(jnp.bfloat16)
    place = lax.broadcasted_iota(jnp.int32, kept.shape, 1) % READ
    left = jnp.where(place == 0, 0.0, pltpu.roll(kept, 1, 1))
    right = jnp.where(place == READ - 1, 0.0, pltpu.roll(kept, size - 1, 1))
    return jnp.concatenate([left, kept, right], axis=0).astype(jnp.bfloat16)


def conv_flat(stack, kernel, out_rows, inside=None, spread=False):
    depth_in, width, lanes_in = stack.shape
    out_depth = depth_in - 2
    out_channels = kernel.shape[2]
    lanes = out_rows * READ
    starts = range(0, lanes, CHUNK)

    def body(s0, s1, s2, w_ref, *refs):
        o_ref = refs[-1]
        sources = (s0, s1, s2)
        for start in starts:
            size = min(CHUNK, lanes - start)
            acc = jnp.zeros((out_channels, size), jnp.float32)
            for dz in range(3):
                for dy in range(3):
                    acc = acc + jnp.dot(
                        w_ref[dz, dy],
                        sources[dz][0, :, pl.ds(start + dy * READ, size)],
                        preferred_element_type=jnp.float32,
                    )
            o_ref[0, :, pl.ds(start, size)] = finish(acc, refs, start, size, spread)

    in_specs = [
        pl.BlockSpec((1, width, lanes_in), lambda z, dz=dz: (z + dz, 0, 0)) for dz in range(3)
    ] + [pl.BlockSpec(kernel.shape, lambda z: (0, 0, 0, 0))]
    extra = ()
    kind = jnp.float32
    stored = 3 * out_channels if spread else out_channels
    if inside is not None:
        in_specs.append(pl.BlockSpec((1, 1, lanes), lambda z: (z, 0, 0)))
        extra = (inside,)
        kind = jnp.bfloat16
    return pl.pallas_call(
        body,
        grid=(out_depth,),
        in_specs=in_specs,
        out_specs=pl.BlockSpec((1, stored, lanes), lambda z: (z, 0, 0)),
        out_shape=jax.ShapeDtypeStruct((out_depth, stored, lanes), kind),
    )(stack, stack, stack, kernel, *extra)


def shifted_stack(block):
    channels = block.shape[1]
    left = jnp.pad(block, ((0, 0), (0, 0), (1, 0)))[..., :-1]
    right = jnp.pad(block, ((0, 0), (0, 0), (0, 1)))[..., 1:]
    place = lax.broadcasted_iota(jnp.int32, block.shape, 2) % READ
    zero = jnp.zeros((), block.dtype)
    left = jnp.where(place == 0, zero, left)
    right = jnp.where(place == READ - 1, zero, right)
    pieces = [left, block, right]
    extra = -(3 * channels) % 16
    if extra:
        pieces.append(jnp.zeros(block.shape[:1] + (extra,) + block.shape[2:], block.dtype))
    return jnp.concatenate(pieces, axis=1)


def kernel_matrix(weight):
    out_channels, in_channels = weight.shape[2], weight.shape[4]
    matrix = weight.reshape(3, 3, out_channels, 3 * in_channels)
    extra_in = -(3 * in_channels) % 16
    extra_out = -out_channels % 8
    return jnp.pad(matrix, ((0, 0), (0, 0), (0, extra_out), (0, extra_in)))


def convolve_flat(block, weight, out_rows, inside=None):
    out = conv_flat(shifted_stack(block), kernel_matrix(weight), out_rows, inside)
    return out[:, : weight.shape[2]]


def conv_roll(block, kernel, out_rows, inside=None):
    depth_in, width, lanes_in = block.shape
    out_depth = depth_in - 2
    out_channels = kernel.shape[2] // 3
    lanes = out_rows * READ
    starts = range(0, lanes, CHUNK)

    def body(s0, s1, s2, w_ref, *refs):
        o_ref = refs[-1]
        sources = (s0, s1, s2)
        for start in starts:
            size = min(CHUNK, lanes - start)
            acc = jnp.zeros((3 * out_channels, size), jnp.float32)
            for dz in range(3):
                for dy in range(3):
                    acc = acc + jnp.dot(
                        w_ref[dz, dy],
                        sources[dz][0, :, pl.ds(start + dy * READ, size)],
                        preferred_element_type=jnp.float32,
                    )
            place = lax.broadcasted_iota(jnp.int32, (out_channels, size), 1) % READ
            left = pltpu.roll(acc[:out_channels], 1, 1)
            right = pltpu.roll(acc[2 * out_channels :], size - 1, 1)
            total = (
                acc[out_channels : 2 * out_channels]
                + jnp.where(place == 0, 0.0, left)
                + jnp.where(place == READ - 1, 0.0, right)
            )
            o_ref[0, :, pl.ds(start, size)] = finish(total, refs, start, size, False)

    in_specs = [
        pl.BlockSpec((1, width, lanes_in), lambda z, dz=dz: (z + dz, 0, 0)) for dz in range(3)
    ] + [pl.BlockSpec(kernel.shape, lambda z: (0, 0, 0, 0))]
    extra = ()
    kind = jnp.float32
    if inside is not None:
        in_specs.append(pl.BlockSpec((1, 1, lanes), lambda z: (z, 0, 0)))
        extra = (inside,)
        kind = jnp.bfloat16
    return pl.pallas_call(
        body,
        grid=(out_depth,),
        in_specs=in_specs,
        out_specs=pl.BlockSpec((1, out_channels, lanes), lambda z: (z, 0, 0)),
        out_shape=jax.ShapeDtypeStruct((out_depth, out_channels, lanes), kind),
    )(block, block, block, kernel, *extra)


def tap_matrix(weight):
    out_channels, in_channels = weight.shape[2], weight.shape[4]
    extra_out = -out_channels % 8
    extra_in = -in_channels % 16
    matrix = jnp.pad(
        weight.transpose(0, 1, 3, 2, 4), ((0, 0), (0, 0), (0, 0), (0, extra_out), (0, extra_in))
    )
    return matrix.reshape(3, 3, 3 * (out_channels + extra_out), in_channels + extra_in)


def padded_channels(block):
    extra = -block.shape[1] % 16
    if extra:
        block = jnp.pad(block, ((0, 0), (0, extra), (0, 0)))
    return block


def convolve_roll(block, weight, out_rows, inside=None):
    out = conv_roll(padded_channels(block), tap_matrix(weight), out_rows, inside)
    return out[:, : weight.shape[2]]


def per_device(
    image_field,
    coil_maps,
    kspace_data,
    sampling_mask,
    consistency_weight,
    conv_first,
    conv_middle,
    conv_last,
):
    slab_rows = image_field.shape[1]
    coil_rows = image_field.shape[2]
    phases = coil_maps.shape[3]
    partitions = kspace_data.shape[2]
    pixels = image_field.astype(jnp.bfloat16)
    sensitivity = coil_maps.astype(jnp.float32)
    values = lax.all_gather(pixels, "coil", axis=2, tiled=True).astype(jnp.float32)[:, None]
    expanded = jnp.stack(
        [
            sensitivity[0] * values[0] - sensitivity[1] * values[1],
            sensitivity[0] * values[1] + sensitivity[1] * values[0],
        ]
    ).astype(jnp.bfloat16)
    spectrum = fourier_section(expanded, 4, False)
    spectrum = fourier_section(spectrum, 3, False)
    spectrum = lax.all_to_all(spectrum, "slab", split_axis=3, concat_axis=2, tiled=True)
    spectrum = fourier_section(spectrum, 2, False)
    weights_mask = sampling_mask.astype(jnp.float32)[None, None, :, :, None]
    residual = (
        weights_mask * (spectrum.astype(jnp.float32) - kspace_data.astype(jnp.float32))
    ).astype(jnp.bfloat16)
    residual = fourier_section(residual, 2, True)
    residual = lax.all_to_all(residual, "slab", split_axis=2, concat_axis=3, tiled=True)
    residual = fourier_section(residual, 3, True)
    restored = fourier_section(residual, 4, True).astype(jnp.float32)
    sensitivity = coil_maps.astype(jnp.float32)
    partial_value = jnp.stack(
        [
            jnp.sum(sensitivity[0] * restored[0] + sensitivity[1] * restored[1], axis=0),
            jnp.sum(sensitivity[0] * restored[1] - sensitivity[1] * restored[0], axis=0),
        ]
    )
    step_size = consistency_weight[0]
    coil_first = lax.axis_index("coil") * coil_rows
    slab_first = lax.axis_index("slab") * slab_rows
    weights = (conv_first, conv_middle, conv_last)
    gathered = lax.all_to_all(
        (-step_size * partial_value).astype(jnp.bfloat16), "coil", 2, 2, tiled=True
    )
    coils = lax.axis_size("coil")
    scattered = jnp.sum(
        gathered.astype(jnp.float32).reshape(2, slab_rows, coils, coil_rows, READ), axis=2
    )
    updated = image_field + scattered
    activations = padded_2(updated.astype(jnp.bfloat16), (("coil", 2),), 3)
    activations = padded_2(activations, (("slab", 1),), 3)
    depth, rows = activations.shape[1], activations.shape[2]
    activations = activations.transpose(1, 0, 2, 3).reshape(depth, 2, rows * READ)
    for layer_index, weight in enumerate(weights):
        rows = rows - 2
        inside = None
        if layer_index < 2:
            margin = 2 - layer_index
            depth_places = slab_first - margin + jnp.arange(depth - 2, dtype=jnp.int32)
            row_places = coil_first - margin + jnp.arange(rows * READ, dtype=jnp.int32) // READ
            inside = (
                ((depth_places >= 0) & (depth_places < partitions))[:, None, None]
                & ((row_places >= 0) & (row_places < phases))[None, None, :]
            ).astype(jnp.float32)
        depth = depth - 2
        if layer_index == 0:
            output = conv_flat(
                shifted_stack(activations), kernel_matrix(weight), rows, inside, spread=True
            )
        elif layer_index == 1:
            output = conv_flat(activations, kernel_matrix(weight), rows, inside)
        else:
            output = convolve_roll(activations, weight, rows, inside)
        activations = output
    correction = output.reshape(slab_rows, 2, coil_rows, READ).transpose(1, 0, 2, 3)
    return updated + correction


def solution(mesh):
    placed = (
        P(None, "slab", "coil", None),
        P(None, "coil", "slab", None, None),
        P(None, "coil", None, "slab", None),
        P(None, "slab"),
        P(),
        P(),
        P(),
        P(),
    )
    return jax.shard_map(
        per_device,
        mesh=mesh,
        in_specs=placed,
        out_specs=P(None, "slab", "coil", None),
        check_vma=False,
    )
```

```python
import math

import jax
import jax.numpy as jnp
from jax import lax
from jax.experimental import pallas as pl
from jax.experimental.pallas import tpu as pltpu
from jax.sharding import PartitionSpec as P


def padded_2(block, sides, width):
    for axis, dim in sides:
        count = lax.axis_size(axis)
        forward = [(i, i + 1) for i in range(count - 1)]
        backward = [(target, source) for source, target in forward]
        low = lax.ppermute(
            lax.slice_in_dim(block, block.shape[dim] - width, None, axis=dim), axis, forward
        )
        high = lax.ppermute(lax.slice_in_dim(block, 0, width, axis=dim), axis, backward)
        block = jnp.concatenate([low, block, high], axis=dim)
    return block


def fourier_tables(length):
    points = jnp.arange(length, dtype=jnp.int32)
    product = points[:, None] * points[None, :] % length
    angles = product.astype(jnp.float32) * (2.0 * math.pi / length)
    scaling = 1.0 / math.sqrt(length)
    return jnp.stack([jnp.cos(angles) * scaling, jnp.sin(angles) * scaling]).astype(jnp.bfloat16)


def fourier_section(values, along, inverse):
    length = values.shape[along]
    tables = fourier_tables(length)
    cosine = tables[0]
    sine = -tables[1] if inverse else tables[1]
    matrix = jnp.stack([jnp.stack([cosine, sine], axis=1), jnp.stack([-sine, cosine], axis=1)])
    result = lax.dot_general(
        matrix, values, (((2, 3), (0, along)), ((), ())), preferred_element_type=jnp.float32
    )
    result = jnp.moveaxis(result, 1, along)
    return result.astype(jnp.bfloat16)


READ = 384
CHUNK = 1536

def finish(total, refs, start, size, spread):
    if len(refs) == 1:
        return total
    keep = refs[0][0, :, pl.ds(start, size)] > 0
    kept = jnp.where(keep, jnp.maximum(total, 0.0), 0.0)
    if not spread:
        return kept.astype(jnp.bfloat16)
    place = lax.broadcasted_iota(jnp.int32, kept.shape, 1) % READ
    left = jnp.where(place == 0, 0.0, pltpu.roll(kept, 1, 1))
    right = jnp.where(place == READ - 1, 0.0, pltpu.roll(kept, size - 1, 1))
    return jnp.concatenate([left, kept, right], axis=0).astype(jnp.bfloat16)


def conv_flat(stack, kernel, out_rows, inside=None, spread=False):
    depth_in, width, lanes_in = stack.shape
    out_depth = depth_in - 2
    out_channels = kernel.shape[2]
    lanes = out_rows * READ
    starts = range(0, lanes, CHUNK)

    def body(s0, s1, s2, w_ref, *refs):
        o_ref = refs[-1]
        sources = (s0, s1, s2)
        for start in starts:
            size = min(CHUNK, lanes - start)
            acc = jnp.zeros((out_channels, size), jnp.float32)
            for dz in range(3):
                for dy in range(3):
                    acc = acc + jnp.dot(
                        w_ref[dz, dy],
                        sources[dz][0, :, pl.ds(start + dy * READ, size)],
                        preferred_element_type=jnp.float32,
                    )
            o_ref[0, :, pl.ds(start, size)] = finish(acc, refs, start, size, spread)

    in_specs = [
        pl.BlockSpec((1, width, lanes_in), lambda z, dz=dz: (z + dz, 0, 0)) for dz in range(3)
    ] + [pl.BlockSpec(kernel.shape, lambda z: (0, 0, 0, 0))]
    extra = ()
    kind = jnp.float32
    stored = 3 * out_channels if spread else out_channels
    if inside is not None:
        in_specs.append(pl.BlockSpec((1, 1, lanes), lambda z: (z, 0, 0)))
        extra = (inside,)
        kind = jnp.bfloat16
    return pl.pallas_call(
        body,
        grid=(out_depth,),
        in_specs=in_specs,
        out_specs=pl.BlockSpec((1, stored, lanes), lambda z: (z, 0, 0)),
        out_shape=jax.ShapeDtypeStruct((out_depth, stored, lanes), kind),
    )(stack, stack, stack, kernel, *extra)


def shifted_stack(block):
    channels = block.shape[1]
    left = jnp.pad(block, ((0, 0), (0, 0), (1, 0)))[..., :-1]
    right = jnp.pad(block, ((0, 0), (0, 0), (0, 1)))[..., 1:]
    place = lax.broadcasted_iota(jnp.int32, block.shape, 2) % READ
    zero = jnp.zeros((), block.dtype)
    left = jnp.where(place == 0, zero, left)
    right = jnp.where(place == READ - 1, zero, right)
    pieces = [left, block, right]
    extra = -(3 * channels) % 16
    if extra:
        pieces.append(jnp.zeros(block.shape[:1] + (extra,) + block.shape[2:], block.dtype))
    return jnp.concatenate(pieces, axis=1)


def kernel_matrix(weight):
    out_channels, in_channels = weight.shape[2], weight.shape[4]
    matrix = weight.reshape(3, 3, out_channels, 3 * in_channels)
    extra_in = -(3 * in_channels) % 16
    extra_out = -out_channels % 8
    return jnp.pad(matrix, ((0, 0), (0, 0), (0, extra_out), (0, extra_in)))


def convolve_flat(block, weight, out_rows, inside=None):
    out = conv_flat(shifted_stack(block), kernel_matrix(weight), out_rows, inside)
    return out[:, : weight.shape[2]]


def conv_roll(block, kernel, out_rows, inside=None):
    depth_in, width, lanes_in = block.shape
    out_depth = depth_in - 2
    out_channels = kernel.shape[2] // 3
    lanes = out_rows * READ
    starts = range(0, lanes, CHUNK)

    def body(s0, s1, s2, w_ref, *refs):
        o_ref = refs[-1]
        sources = (s0, s1, s2)
        for start in starts:
            size = min(CHUNK, lanes - start)
            acc = jnp.zeros((3 * out_channels, size), jnp.float32)
            for dz in range(3):
                for dy in range(3):
                    acc = acc + jnp.dot(
                        w_ref[dz, dy],
                        sources[dz][0, :, pl.ds(start + dy * READ, size)],
                        preferred_element_type=jnp.float32,
                    )
            place = lax.broadcasted_iota(jnp.int32, (out_channels, size), 1) % READ
            left = pltpu.roll(acc[:out_channels], 1, 1)
            right = pltpu.roll(acc[2 * out_channels :], size - 1, 1)
            total = (
                acc[out_channels : 2 * out_channels]
                + jnp.where(place == 0, 0.0, left)
                + jnp.where(place == READ - 1, 0.0, right)
            )
            o_ref[0, :, pl.ds(start, size)] = finish(total, refs, start, size, False)

    in_specs = [
        pl.BlockSpec((1, width, lanes_in), lambda z, dz=dz: (z + dz, 0, 0)) for dz in range(3)
    ] + [pl.BlockSpec(kernel.shape, lambda z: (0, 0, 0, 0))]
    extra = ()
    kind = jnp.float32
    if inside is not None:
        in_specs.append(pl.BlockSpec((1, 1, lanes), lambda z: (z, 0, 0)))
        extra = (inside,)
        kind = jnp.bfloat16
    return pl.pallas_call(
        body,
        grid=(out_depth,),
        in_specs=in_specs,
        out_specs=pl.BlockSpec((1, out_channels, lanes), lambda z: (z, 0, 0)),
        out_shape=jax.ShapeDtypeStruct((out_depth, out_channels, lanes), kind),
    )(block, block, block, kernel, *extra)


def tap_matrix(weight):
    out_channels, in_channels = weight.shape[2], weight.shape[4]
    extra_out = -out_channels % 8
    extra_in = -in_channels % 16
    matrix = jnp.pad(
        weight.transpose(0, 1, 3, 2, 4), ((0, 0), (0, 0), (0, 0), (0, extra_out), (0, extra_in))
    )
    return matrix.reshape(3, 3, 3 * (out_channels + extra_out), in_channels + extra_in)


def padded_channels(block):
    extra = -block.shape[1] % 16
    if extra:
        block = jnp.pad(block, ((0, 0), (0, extra), (0, 0)))
    return block


def convolve_roll(block, weight, out_rows, inside=None):
    out = conv_roll(padded_channels(block), tap_matrix(weight), out_rows, inside)
    return out[:, : weight.shape[2]]


def halo_both(block, width):
    coils = lax.axis_size("coil")
    slabs = lax.axis_size("slab")

    def moved(piece, coil_step, slab_step):
        pairs = []
        for coil in range(coils):
            for slab in range(slabs):
                target_coil, target_slab = coil + coil_step, slab + slab_step
                if 0 <= target_coil < coils and 0 <= target_slab < slabs:
                    pairs.append((coil * slabs + slab, target_coil * slabs + target_slab))
        return lax.ppermute(piece, ("coil", "slab"), pairs)

    depth, rows = block.shape[1], block.shape[2]
    rows_of = {1: (rows - width, rows), 0: (0, rows), -1: (0, width)}
    depth_of = {1: (depth - width, depth), 0: (0, depth), -1: (0, width)}
    grid = []
    for slab_step in (1, 0, -1):
        line = []
        for coil_step in (1, 0, -1):
            low_z, high_z = depth_of[slab_step]
            low_y, high_y = rows_of[coil_step]
            piece = block[:, low_z:high_z, low_y:high_y]
            if coil_step or slab_step:
                piece = moved(piece, coil_step, slab_step)
            line.append(piece)
        grid.append(jnp.concatenate(line, axis=2))
    return jnp.concatenate(grid, axis=1)


def per_device(
    image_field,
    coil_maps,
    kspace_data,
    sampling_mask,
    consistency_weight,
    conv_first,
    conv_middle,
    conv_last,
):
    slab_rows = image_field.shape[1]
    coil_rows = image_field.shape[2]
    phases = coil_maps.shape[3]
    partitions = kspace_data.shape[2]
    pixels = image_field.astype(jnp.bfloat16)
    sensitivity = coil_maps.astype(jnp.float32)
    values = lax.all_gather(pixels, "coil", axis=2, tiled=True).astype(jnp.float32)[:, None]
    expanded = jnp.stack(
        [
            sensitivity[0] * values[0] - sensitivity[1] * values[1],
            sensitivity[0] * values[1] + sensitivity[1] * values[0],
        ]
    ).astype(jnp.bfloat16)
    spectrum = fourier_section(expanded, 4, False)
    spectrum = fourier_section(spectrum, 3, False)
    spectrum = lax.all_to_all(spectrum, "slab", split_axis=3, concat_axis=2, tiled=True)
    spectrum = fourier_section(spectrum, 2, False)
    weights_mask = sampling_mask.astype(jnp.float32)[None, None, :, :, None]
    residual = (
        weights_mask * (spectrum.astype(jnp.float32) - kspace_data.astype(jnp.float32))
    ).astype(jnp.bfloat16)
    residual = fourier_section(residual, 2, True)
    residual = lax.all_to_all(residual, "slab", split_axis=2, concat_axis=3, tiled=True)
    residual = fourier_section(residual, 3, True)
    restored = fourier_section(residual, 4, True).astype(jnp.float32)
    sensitivity = coil_maps.astype(jnp.float32)
    partial_value = jnp.stack(
        [
            jnp.sum(sensitivity[0] * restored[0] + sensitivity[1] * restored[1], axis=0),
            jnp.sum(sensitivity[0] * restored[1] - sensitivity[1] * restored[0], axis=0),
        ]
    )
    step_size = consistency_weight[0]
    coil_first = lax.axis_index("coil") * coil_rows
    slab_first = lax.axis_index("slab") * slab_rows
    weights = (conv_first, conv_middle, conv_last)
    gathered = lax.all_to_all(
        (-step_size * partial_value).astype(jnp.bfloat16), "coil", 2, 2, tiled=True
    )
    coils = lax.axis_size("coil")
    scattered = jnp.sum(
        gathered.astype(jnp.float32).reshape(2, slab_rows, coils, coil_rows, READ), axis=2
    )
    updated = image_field + scattered
    activations = halo_both(updated.astype(jnp.bfloat16), 3)
    depth, rows = activations.shape[1], activations.shape[2]
    activations = activations.transpose(1, 0, 2, 3).reshape(depth, 2, rows * READ)
    for layer_index, weight in enumerate(weights):
        rows = rows - 2
        inside = None
        if layer_index < 2:
            margin = 2 - layer_index
            depth_places = slab_first - margin + jnp.arange(depth - 2, dtype=jnp.int32)
            row_places = coil_first - margin + jnp.arange(rows * READ, dtype=jnp.int32) // READ
            inside = (
                ((depth_places >= 0) & (depth_places < partitions))[:, None, None]
                & ((row_places >= 0) & (row_places < phases))[None, None, :]
            ).astype(jnp.float32)
        depth = depth - 2
        if layer_index == 0:
            output = conv_flat(
                shifted_stack(activations), kernel_matrix(weight), rows, inside, spread=True
            )
        elif layer_index == 1:
            output = conv_flat(activations, kernel_matrix(weight), rows, inside)
        else:
            output = convolve_roll(activations, weight, rows, inside)
        activations = output
    correction = output.reshape(slab_rows, 2, coil_rows, READ).transpose(1, 0, 2, 3)
    return updated + correction


def solution(mesh):
    placed = (
        P(None, "slab", "coil", None),
        P(None, "coil", "slab", None, None),
        P(None, "coil", None, "slab", None),
        P(None, "slab"),
        P(),
        P(),
        P(),
        P(),
    )
    return jax.shard_map(
        per_device,
        mesh=mesh,
        in_specs=placed,
        out_specs=P(None, "slab", "coil", None),
        check_vma=False,
    )
```

```python
import math

import jax
import jax.numpy as jnp
from jax import lax
from jax.experimental import pallas as pl
from jax.experimental.pallas import tpu as pltpu
from jax.sharding import PartitionSpec as P


def padded_2(block, sides, width):
    for axis, dim in sides:
        count = lax.axis_size(axis)
        forward = [(i, i + 1) for i in range(count - 1)]
        backward = [(target, source) for source, target in forward]
        low = lax.ppermute(
            lax.slice_in_dim(block, block.shape[dim] - width, None, axis=dim), axis, forward
        )
        high = lax.ppermute(lax.slice_in_dim(block, 0, width, axis=dim), axis, backward)
        block = jnp.concatenate([low, block, high], axis=dim)
    return block


def fourier_tables(length):
    points = jnp.arange(length, dtype=jnp.int32)
    product = points[:, None] * points[None, :] % length
    angles = product.astype(jnp.float32) * (2.0 * math.pi / length)
    scaling = 1.0 / math.sqrt(length)
    return jnp.stack([jnp.cos(angles) * scaling, jnp.sin(angles) * scaling]).astype(jnp.bfloat16)


def fourier_section(values, along, inverse):
    length = values.shape[along]
    tables = fourier_tables(length)
    cosine = tables[0]
    sine = -tables[1] if inverse else tables[1]
    matrix = jnp.stack([jnp.stack([cosine, sine], axis=1), jnp.stack([-sine, cosine], axis=1)])
    result = lax.dot_general(
        matrix, values, (((2, 3), (0, along)), ((), ())), preferred_element_type=jnp.float32
    )
    result = jnp.moveaxis(result, 1, along)
    return result.astype(jnp.bfloat16)


READ = 384
CHUNK = 1536

def finish(total, refs, start, size, spread):
    if len(refs) == 1:
        return total
    keep = refs[0][0, :, pl.ds(start, size)] > 0
    kept = jnp.where(keep, jnp.maximum(total, 0.0), 0.0)
    if not spread:
        return kept.astype(jnp.bfloat16)
    place = lax.broadcasted_iota(jnp.int32, kept.shape, 1) % READ
    left = jnp.where(place == 0, 0.0, pltpu.roll(kept, 1, 1))
    right = jnp.where(place == READ - 1, 0.0, pltpu.roll(kept, size - 1, 1))
    return jnp.concatenate([left, kept, right], axis=0).astype(jnp.bfloat16)


def conv_flat(stack, kernel, out_rows, inside=None, spread=False):
    depth_in, width, lanes_in = stack.shape
    out_depth = depth_in - 2
    out_channels = kernel.shape[2]
    lanes = out_rows * READ
    starts = range(0, lanes, CHUNK)

    def body(s0, s1, s2, w_ref, *refs):
        o_ref = refs[-1]
        sources = (s0, s1, s2)
        for start in starts:
            size = min(CHUNK, lanes - start)
            acc = jnp.zeros((out_channels, size), jnp.float32)
            for dz in range(3):
                for dy in range(3):
                    acc = acc + jnp.dot(
                        w_ref[dz, dy],
                        sources[dz][0, :, pl.ds(start + dy * READ, size)],
                        preferred_element_type=jnp.float32,
                    )
            o_ref[0, :, pl.ds(start, size)] = finish(acc, refs, start, size, spread)

    in_specs = [
        pl.BlockSpec((1, width, lanes_in), lambda z, dz=dz: (z + dz, 0, 0)) for dz in range(3)
    ] + [pl.BlockSpec(kernel.shape, lambda z: (0, 0, 0, 0))]
    extra = ()
    kind = jnp.float32
    stored = 3 * out_channels if spread else out_channels
    if inside is not None:
        in_specs.append(pl.BlockSpec((1, 1, lanes), lambda z: (z, 0, 0)))
        extra = (inside,)
        kind = jnp.bfloat16
    return pl.pallas_call(
        body,
        grid=(out_depth,),
        in_specs=in_specs,
        out_specs=pl.BlockSpec((1, stored, lanes), lambda z: (z, 0, 0)),
        out_shape=jax.ShapeDtypeStruct((out_depth, stored, lanes), kind),
    )(stack, stack, stack, kernel, *extra)


def shifted_stack(block):
    channels = block.shape[1]
    left = jnp.pad(block, ((0, 0), (0, 0), (1, 0)))[..., :-1]
    right = jnp.pad(block, ((0, 0), (0, 0), (0, 1)))[..., 1:]
    place = lax.broadcasted_iota(jnp.int32, block.shape, 2) % READ
    zero = jnp.zeros((), block.dtype)
    left = jnp.where(place == 0, zero, left)
    right = jnp.where(place == READ - 1, zero, right)
    pieces = [left, block, right]
    extra = -(3 * channels) % 16
    if extra:
        pieces.append(jnp.zeros(block.shape[:1] + (extra,) + block.shape[2:], block.dtype))
    return jnp.concatenate(pieces, axis=1)


def kernel_matrix(weight):
    out_channels, in_channels = weight.shape[2], weight.shape[4]
    matrix = weight.reshape(3, 3, out_channels, 3 * in_channels)
    extra_in = -(3 * in_channels) % 16
    extra_out = -out_channels % 8
    return jnp.pad(matrix, ((0, 0), (0, 0), (0, extra_out), (0, extra_in)))


def convolve_flat(block, weight, out_rows, inside=None):
    out = conv_flat(shifted_stack(block), kernel_matrix(weight), out_rows, inside)
    return out[:, : weight.shape[2]]


def conv_roll(block, kernel, out_rows, inside=None, kept=None):
    depth_in, width, lanes_in = block.shape
    out_depth = depth_in - 2
    out_channels = kernel.shape[2] // 3
    kept = kept or out_channels
    lanes = out_rows * READ
    starts = range(0, lanes, CHUNK)

    def body(s0, s1, s2, w_ref, *refs):
        o_ref = refs[-1]
        sources = (s0, s1, s2)
        for start in starts:
            size = min(CHUNK, lanes - start)
            acc = jnp.zeros((3 * out_channels, size), jnp.float32)
            for dz in range(3):
                for dy in range(3):
                    acc = acc + jnp.dot(
                        w_ref[dz, dy],
                        sources[dz][0, :, pl.ds(start + dy * READ, size)],
                        preferred_element_type=jnp.float32,
                    )
            place = lax.broadcasted_iota(jnp.int32, (out_channels, size), 1) % READ
            left = pltpu.roll(acc[:out_channels], 1, 1)
            right = pltpu.roll(acc[2 * out_channels :], size - 1, 1)
            total = (
                acc[out_channels : 2 * out_channels]
                + jnp.where(place == 0, 0.0, left)
                + jnp.where(place == READ - 1, 0.0, right)
            )
            o_ref[0, :, pl.ds(start, size)] = finish(total[:kept], refs, start, size, False)

    in_specs = [
        pl.BlockSpec((1, width, lanes_in), lambda z, dz=dz: (z + dz, 0, 0)) for dz in range(3)
    ] + [pl.BlockSpec(kernel.shape, lambda z: (0, 0, 0, 0))]
    extra = ()
    kind = jnp.float32
    if inside is not None:
        in_specs.append(pl.BlockSpec((1, 1, lanes), lambda z: (z, 0, 0)))
        extra = (inside,)
        kind = jnp.bfloat16
    return pl.pallas_call(
        body,
        grid=(out_depth,),
        in_specs=in_specs,
        out_specs=pl.BlockSpec((1, kept, lanes), lambda z: (z, 0, 0)),
        out_shape=jax.ShapeDtypeStruct((out_depth, kept, lanes), kind),
    )(block, block, block, kernel, *extra)


def tap_matrix(weight):
    out_channels, in_channels = weight.shape[2], weight.shape[4]
    extra_out = -out_channels % 8
    extra_in = -in_channels % 16
    matrix = jnp.pad(
        weight.transpose(0, 1, 3, 2, 4), ((0, 0), (0, 0), (0, 0), (0, extra_out), (0, extra_in))
    )
    return matrix.reshape(3, 3, 3 * (out_channels + extra_out), in_channels + extra_in)


def padded_channels(block):
    extra = -block.shape[1] % 16
    if extra:
        block = jnp.pad(block, ((0, 0), (0, extra), (0, 0)))
    return block


def convolve_roll(block, weight, out_rows, inside=None):
    out = conv_roll(padded_channels(block), tap_matrix(weight), out_rows, inside, weight.shape[2])
    return out[:, : weight.shape[2]]


def per_device(
    image_field,
    coil_maps,
    kspace_data,
    sampling_mask,
    consistency_weight,
    conv_first,
    conv_middle,
    conv_last,
):
    slab_rows = image_field.shape[1]
    coil_rows = image_field.shape[2]
    phases = coil_maps.shape[3]
    partitions = kspace_data.shape[2]
    pixels = image_field.astype(jnp.bfloat16)
    sensitivity = coil_maps.astype(jnp.float32)
    values = lax.all_gather(pixels, "coil", axis=2, tiled=True).astype(jnp.float32)[:, None]
    expanded = jnp.stack(
        [
            sensitivity[0] * values[0] - sensitivity[1] * values[1],
            sensitivity[0] * values[1] + sensitivity[1] * values[0],
        ]
    ).astype(jnp.bfloat16)
    spectrum = fourier_section(expanded, 4, False)
    spectrum = fourier_section(spectrum, 3, False)
    spectrum = lax.all_to_all(spectrum, "slab", split_axis=3, concat_axis=2, tiled=True)
    spectrum = fourier_section(spectrum, 2, False)
    weights_mask = sampling_mask.astype(jnp.float32)[None, None, :, :, None]
    residual = (
        weights_mask * (spectrum.astype(jnp.float32) - kspace_data.astype(jnp.float32))
    ).astype(jnp.bfloat16)
    residual = fourier_section(residual, 2, True)
    residual = lax.all_to_all(residual, "slab", split_axis=2, concat_axis=3, tiled=True)
    residual = fourier_section(residual, 3, True)
    restored = fourier_section(residual, 4, True).astype(jnp.float32)
    sensitivity = coil_maps.astype(jnp.float32)
    partial_value = jnp.stack(
        [
            jnp.sum(sensitivity[0] * restored[0] + sensitivity[1] * restored[1], axis=0),
            jnp.sum(sensitivity[0] * restored[1] - sensitivity[1] * restored[0], axis=0),
        ]
    )
    step_size = consistency_weight[0]
    coil_first = lax.axis_index("coil") * coil_rows
    slab_first = lax.axis_index("slab") * slab_rows
    weights = (conv_first, conv_middle, conv_last)
    gathered = lax.all_to_all(
        (-step_size * partial_value).astype(jnp.bfloat16), "coil", 2, 2, tiled=True
    )
    coils = lax.axis_size("coil")
    scattered = jnp.sum(
        gathered.astype(jnp.float32).reshape(2, slab_rows, coils, coil_rows, READ), axis=2
    )
    updated = image_field + scattered
    activations = padded_2(updated.astype(jnp.bfloat16), (("coil", 2),), 3)
    activations = padded_2(activations, (("slab", 1),), 3)
    depth, rows = activations.shape[1], activations.shape[2]
    activations = activations.transpose(1, 0, 2, 3).reshape(depth, 2, rows * READ)
    for layer_index, weight in enumerate(weights):
        rows = rows - 2
        inside = None
        if layer_index < 2:
            margin = 2 - layer_index
            depth_places = slab_first - margin + jnp.arange(depth - 2, dtype=jnp.int32)
            row_places = coil_first - margin + jnp.arange(rows * READ, dtype=jnp.int32) // READ
            inside = (
                ((depth_places >= 0) & (depth_places < partitions))[:, None, None]
                & ((row_places >= 0) & (row_places < phases))[None, None, :]
            ).astype(jnp.float32)
        depth = depth - 2
        if layer_index == 0:
            output = conv_flat(
                shifted_stack(activations), kernel_matrix(weight), rows, inside, spread=True
            )
        elif layer_index == 1:
            output = conv_flat(activations, kernel_matrix(weight), rows, inside)
        else:
            output = convolve_roll(activations, weight, rows, inside)
        activations = output
    correction = output.reshape(slab_rows, 2, coil_rows, READ).transpose(1, 0, 2, 3)
    return updated + correction


def solution(mesh):
    placed = (
        P(None, "slab", "coil", None),
        P(None, "coil", "slab", None, None),
        P(None, "coil", None, "slab", None),
        P(None, "slab"),
        P(),
        P(),
        P(),
        P(),
    )
    return jax.shard_map(
        per_device,
        mesh=mesh,
        in_specs=placed,
        out_specs=P(None, "slab", "coil", None),
        check_vma=False,
    )
```
